32 devices in a mesh: groups: 2 (over y), dp: 4 (over z), task: 4 (over x, core).
Axes of the slice: x: 2, y: 2, z: 4, core: 2. Of those that a mesh axis runs over, the one named last changes fastest.
Arguments:
- coords: bfloat16 [3, 6144], P(None, ('groups', 'dp')), parts along dimension 1, may hold values from 0 to 1
- lengthscales: float32 [6], P('groups'), parts along dimension 0, may hold values from 0.15 to 0.5
- vectors: bfloat16 [2, 6144, 256], P(None, ('groups', 'dp'), 'task'), parts along dimension 1, may hold values from -6 to 6
- mixing: bfloat16 [512, 256], P('groups'), parts along dimension 0, may hold values from -0.078125 to 0.078125
- noise: float32 [512], P(('groups', 'task')), parts along dimension 0, may hold values from 0.1 to 1
Outputs:
- product: bfloat16 [2, 6144, 256], P(None, ('groups', 'dp'), 'task'), parts along dimension 1
- gradient: float32 [512, 256], P(('groups', 'task')), parts along dimension 0
The draws below stay inside these ranges and needn't reach their ends.
There are 2 independent parts, one for each index of `groups`. The reference program is written for one: setup_inputs(seed, part) draws one part's arguments, and reference() takes and returns one part's arrays. A program takes and returns all parts, laid end to end along the dimension named above; each array names one. Nothing has to cross between parts.
All inputs are finite; a program needn't handle non-finite values.
Results may differ from the reference program's by a relative error of at most 0.0056.
Values may be sent and summed in bfloat16 or wider, within the bound.
No kernel may reach another device: no remote copies, remote signals or barrier semaphores. Data moves between devices by JAX's collectives and lax.ppermute only.
A program may use at most 64 MiB of HBM per device.

```python
import math
import jax
import jax.numpy as jnp
from jax import lax

M = 256
DIN = 3
NX = 3072


def block_scale(own_key, extent, split, least, largest):
    factor_of = 1.0
    for axis_at, parts in split:
        heights = jax.random.uniform(jax.random.fold_in(jax.random.fold_in(own_key, 6), axis_at), (parts,), jnp.float32, least / len(split), largest / len(split))
        factor_of = factor_of * jnp.repeat(jnp.exp(heights), extent[axis_at] // parts).reshape((-1,) + (1,) * (len(extent) - 1 - axis_at))
    return factor_of


def scatter_about(own_key, shape, deviation, bound, split=(), kind=jnp.bfloat16):
    values = deviation * jax.random.normal(own_key, shape, jnp.float32)
    if split:
        values = values * block_scale(own_key, shape, split, -0.22, 0.18)
    return jnp.clip(values, -bound, bound).astype(kind)


def setup_inputs(seed: int = 0, part: int = 0) -> dict:
    seeds = jax.random.split(jax.random.key(seed), 6)
    part_keys = jax.random.split(jax.random.fold_in(seeds[5], part), 6)
    coords = jnp.clip(1.0 * jax.random.uniform(part_keys[0], (DIN, NX), jnp.float32) ** block_scale(part_keys[0], (DIN, NX), ((1, 4),), -0.2, 0.2), 0.0, 1.0).astype(jnp.bfloat16)
    lengthscales = jnp.clip(jnp.exp(jax.random.uniform(part_keys[1], (DIN,), jnp.float32, math.log(0.15), math.log(0.5))), 0.15, 0.5)
    vectors = scatter_about(part_keys[2], (2, NX, M), 1.0, 6.0, ((1, 4), (2, 4)))
    mixing = scatter_about(part_keys[3], (M, M), (0.3 / NX ** 0.5), 0.078125)
    noise = jnp.clip(jnp.exp(math.log(1.0) - 2.3025851 * jax.random.uniform(part_keys[4], (M,), jnp.float32) ** block_scale(part_keys[4], (M,), ((0, 4),), -0.2, 0.2)), 0.1, 1.0)
    return dict(coords=coords, lengthscales=lengthscales, vectors=vectors, mixing=mixing, noise=noise)


def kernel_tile(left, right):
    diff = left[:, :, None] - right[:, None, :]
    return jnp.exp(0.1 - jnp.sqrt(lax.optimization_barrier(jnp.sum(diff * diff, axis=0)) + 0.01))

def reference(coords, lengthscales, vectors, mixing, noise):
    inverse = 1.0 / lengthscales
    scaled = coords.astype(jnp.float32) * inverse[:, None]
    block = math.gcd(NX, 512)
    count = NX // block
    vec32 = vectors.astype(jnp.float32)

    def one_block(index):
        left = lax.dynamic_slice_in_dim(scaled, index * block, block, 1)
        tile = kernel_tile(left, scaled).astype(jnp.bfloat16).astype(jnp.float32)
        return jnp.einsum('nr,srm->snm', tile, vec32)
    blocks = lax.map(one_block, jnp.arange(count, dtype=jnp.int32))
    images = jnp.transpose(blocks, (1, 0, 2, 3)).reshape(2, NX, M).astype(jnp.bfloat16)
    img32 = images.astype(jnp.float32)
    mixed = jnp.einsum('sna,ca->snc', img32, mixing.astype(jnp.float32))
    product = (mixed + noise[None, None, :] * vec32).astype(jnp.bfloat16)
    first = jnp.einsum('na,nb->ab', img32[0], vec32[0])
    second = jnp.einsum('na,nb->ab', img32[1], vec32[1])
    gradient = (first - second) / (2.0 * NX)
    return (product, gradient)
```

```python
import jax
import jax.numpy as jnp
from jax import lax
from jax.sharding import PartitionSpec as P


def kernel_tile(left, right):
    diff = left[:, :, None] - right[:, None, :]
    return jnp.exp(0.1 - jnp.sqrt(jnp.sum(diff * diff, axis=0) + 0.01))


def shift(x, axis, k, n):
    return lax.ppermute(x, axis, [(i, (i + k) % n) for i in range(n)])


def butterfly_sum(x, axis, n):
    if n & (n - 1):
        return lax.psum(x, axis)
    step = 1
    while step < n:
        x = x + lax.ppermute(x, axis, [(i, i ^ step) for i in range(n)])
        step *= 2
    return x


def per_device(coords, lengthscales, vectors, mixing, noise):
    n_rows = coords.shape[1]
    local_tasks = vectors.shape[2]
    n_dp = lax.axis_size("dp")
    inverse = 1.0 / lengthscales
    own_scaled = coords.astype(jnp.float32) * inverse[:, None]
    task_start = lax.axis_index("task") * local_tasks

    def block(right_coords, values):
        right = right_coords.astype(jnp.float32) * inverse[:, None]
        tile = kernel_tile(own_scaled, right).astype(jnp.bfloat16)
        return jnp.einsum("nr,srm->snm", tile, values, preferred_element_type=jnp.float32)

    summed = block(coords, vectors)
    if n_dp <= 4:
        for k in range(1, n_dp):
            summed = summed + block(shift(coords, "dp", k, n_dp), shift(vectors, "dp", k, n_dp))
    else:

        def ring(_, carry):
            accum, right_coords, values = carry
            right_coords = shift(right_coords, "dp", 1, n_dp)
            values = shift(values, "dp", 1, n_dp)
            return accum + block(right_coords, values), right_coords, values

        summed = lax.fori_loop(0, n_dp - 1, ring, (summed, coords, vectors))[0]
    whole_vectors = lax.all_gather(vectors, "task", axis=2, tiled=True)
    images = summed.astype(jnp.bfloat16)
    whole_images = lax.all_gather(images, "task", axis=2, tiled=True)
    own_rows = lax.dynamic_slice_in_dim(mixing, task_start, local_tasks, 0)
    mixed = jnp.einsum("sna,ca->snc", whole_images, own_rows, preferred_element_type=jnp.float32)
    product = (mixed + noise[None, None, :] * vectors.astype(jnp.float32)).astype(jnp.bfloat16)
    signs = jnp.array([1.0, -1.0], jnp.bfloat16)
    signed = images * signs[:, None, None]
    partial_grad = jnp.einsum(
        "sna,snb->ab", signed, whole_vectors, preferred_element_type=jnp.float32
    )
    total = butterfly_sum(partial_grad, "dp", n_dp)
    gradient = total / (2.0 * n_rows * n_dp)
    return (product, gradient)


def solution(mesh):
    in_specs = (
        P(None, ("groups", "dp")),
        P("groups"),
        P(None, ("groups", "dp"), "task"),
        P("groups", None),
        P(("groups", "task")),
    )
    out_specs = (P(None, ("groups", "dp"), "task"), P(("groups", "task"), None))
    return jax.shard_map(
        per_device, mesh=mesh, in_specs=in_specs, out_specs=out_specs, check_vma=False
    )
```

```python
import jax
import jax.numpy as jnp
from jax import lax
from jax.sharding import PartitionSpec as P


def kernel_tile(left, right):
    diff = left[:, :, None] - right[:, None, :]
    return jnp.exp(0.1 - jnp.sqrt(jnp.sum(diff * diff, axis=0) + 0.01))


def shift(x, axis, k, n):
    return lax.ppermute(x, axis, [(i, (i + k) % n) for i in range(n)])


def sum_over(x, axis, n):
    if n == 4:
        got = [shift(x, axis, k, n) for k in range(1, n)]
        even = lax.axis_index(axis) % 2 == 0
        first = x + jnp.where(even, got[2], got[0])
        second = got[1] + jnp.where(even, got[0], got[2])
        return first + second
    if n & (n - 1):
        return lax.psum(x, axis)
    step = 1
    while step < n:
        x = x + lax.ppermute(x, axis, [(i, i ^ step) for i in range(n)])
        step *= 2
    return x


def per_device(coords, lengthscales, vectors, mixing, noise):
    n_rows = coords.shape[1]
    local_tasks = vectors.shape[2]
    n_dp = lax.axis_size("dp")
    n_task = lax.axis_size("task")
    task_index = lax.axis_index("task")
    inverse = 1.0 / lengthscales
    own_scaled = coords.astype(jnp.float32) * inverse[:, None]
    task_start = task_index * local_tasks

    def block(right_coords, values):
        right = right_coords.astype(jnp.float32) * inverse[:, None]
        tile = kernel_tile(own_scaled, right).astype(jnp.bfloat16)
        return jnp.einsum("nr,srm->snm", tile, values, preferred_element_type=jnp.float32)

    summed = block(coords, vectors)
    if n_dp <= 4:
        for k in range(1, n_dp):
            summed = summed + block(shift(coords, "dp", k, n_dp), shift(vectors, "dp", k, n_dp))
    else:

        def ring(_, carry):
            accum, right_coords, values = carry
            right_coords = shift(right_coords, "dp", 1, n_dp)
            values = shift(values, "dp", 1, n_dp)
            return accum + block(right_coords, values), right_coords, values

        summed = lax.fori_loop(0, n_dp - 1, ring, (summed, coords, vectors))[0]

    task_blocks = [(task_index, vectors)]
    for k in range(1, n_task):
        task_blocks.append(((task_index - k) % n_task, shift(vectors, "task", k, n_task)))
    images = summed.astype(jnp.bfloat16)
    whole_images = lax.all_gather(images, "task", axis=2, tiled=True)
    own_rows = lax.dynamic_slice_in_dim(mixing, task_start, local_tasks, 0)
    mixed = jnp.einsum("sna,ca->snc", whole_images, own_rows, preferred_element_type=jnp.float32)
    product = (mixed + noise[None, None, :] * vectors.astype(jnp.float32)).astype(jnp.bfloat16)
    signs = jnp.array([1.0, -1.0], jnp.bfloat16)
    signed = images * signs[:, None, None]
    partial_grad = jnp.zeros((local_tasks, n_task * local_tasks), jnp.float32)
    for source, values in task_blocks:
        piece = jnp.einsum("sna,snb->ab", signed, values, preferred_element_type=jnp.float32)
        partial_grad = lax.dynamic_update_slice_in_dim(
            partial_grad, piece, source * local_tasks, 1
        )
    total = sum_over(partial_grad, "dp", n_dp)
    gradient = total / (2.0 * n_rows * n_dp)
    return (product, gradient)


def solution(mesh):
    in_specs = (
        P(None, ("groups", "dp")),
        P("groups"),
        P(None, ("groups", "dp"), "task"),
        P("groups", None),
        P(("groups", "task")),
    )
    out_specs = (P(None, ("groups", "dp"), "task"), P(("groups", "task"), None))
    return jax.shard_map(
        per_device, mesh=mesh, in_specs=in_specs, out_specs=out_specs, check_vma=False
    )
```

```python
import jax
import jax.numpy as jnp
from jax import lax
from jax.sharding import PartitionSpec as P


def kernel_tile(left, right):
    diff = left[:, :, None] - right[:, None, :]
    return jnp.exp(0.1 - jnp.sqrt(jnp.sum(diff * diff, axis=0) + 0.01))


def shift(x, axis, k, n):
    return lax.ppermute(x, axis, [(i, (i + k) % n) for i in range(n)])


def sum_over(x, axis, n):
    if n == 4:
        got = [shift(x, axis, k, n) for k in range(1, n)]
        even = lax.axis_index(axis) % 2 == 0
        first = x + jnp.where(even, got[2], got[0])
        second = got[1] + jnp.where(even, got[0], got[2])
        return first + second
    if n & (n - 1):
        return lax.psum(x, axis)
    step = 1
    while step < n:
        x = x + lax.ppermute(x, axis, [(i, i ^ step) for i in range(n)])
        step *= 2
    return x


def rows_to_owner(columns, axis, n, width):
    me = lax.axis_index(axis)
    pieces = []
    for k in range(n):
        rows = lax.dynamic_slice_in_dim(columns, ((me - k) % n) * width, width, 0)
        pieces.append(rows if k == 0 else shift(rows, axis, -k, n))
    ordered = jnp.concatenate(pieces + pieces, axis=1)
    return lax.dynamic_slice_in_dim(ordered, ((n - me) % n) * width, n * width, 1)


def per_device(coords, lengthscales, vectors, mixing, noise):
    n_rows = coords.shape[1]
    local_tasks = vectors.shape[2]
    n_dp = lax.axis_size("dp")
    n_task = lax.axis_size("task")
    task_start = lax.axis_index("task") * local_tasks
    inverse = 1.0 / lengthscales
    own_scaled = coords.astype(jnp.float32) * inverse[:, None]

    def block(right_coords, values):
        right = right_coords.astype(jnp.float32) * inverse[:, None]
        tile = kernel_tile(own_scaled, right).astype(jnp.bfloat16)
        return jnp.einsum("nr,srm->snm", tile, values, preferred_element_type=jnp.float32)

    summed = block(coords, vectors)
    if n_dp <= 4:
        moved = [shift(vectors, "dp", k, n_dp) for k in range(1, n_dp)]
        for k in range(1, n_dp):
            summed = summed + block(shift(coords, "dp", k, n_dp), moved[k - 1])
    else:

        def ring(_, carry):
            accum, right_coords, values = carry
            right_coords = shift(right_coords, "dp", 1, n_dp)
            values = shift(values, "dp", 1, n_dp)
            return accum + block(right_coords, values), right_coords, values

        summed = lax.fori_loop(0, n_dp - 1, ring, (summed, coords, vectors))[0]

    images = summed.astype(jnp.bfloat16)
    whole_images = lax.all_gather(images, "task", axis=2, tiled=True)
    own_rows = lax.dynamic_slice_in_dim(mixing, task_start, local_tasks, 0)
    mixed = jnp.einsum("sna,ca->snc", whole_images, own_rows, preferred_element_type=jnp.float32)
    product = (mixed + noise[None, None, :] * vectors.astype(jnp.float32)).astype(jnp.bfloat16)
    signs = jnp.array([1.0, -1.0], jnp.bfloat16)
    signed = vectors * signs[:, None, None]
    columns = jnp.einsum(
        "sna,snb->ab", whole_images, signed, preferred_element_type=jnp.float32
    )
    columns = sum_over(columns, "dp", n_dp)
    total = rows_to_owner(columns, "task", n_task, local_tasks)
    gradient = total / (2.0 * n_rows * n_dp)
    return (product, gradient)


def solution(mesh):
    in_specs = (
        P(None, ("groups", "dp")),
        P("groups"),
        P(None, ("groups", "dp"), "task"),
        P("groups", None),
        P(("groups", "task")),
    )
    out_specs = (P(None, ("groups", "dp"), "task"), P(("groups", "task"), None))
    return jax.shard_map(
        per_device, mesh=mesh, in_specs=in_specs, out_specs=out_specs, check_vma=False
    )
```

```python
import jax
import jax.numpy as jnp
from jax import lax
from jax.sharding import PartitionSpec as P


def kernel_tile(left, right):
    diff = left[:, :, None] - right[:, None, :]
    return jnp.exp(0.1 - jnp.sqrt(jnp.sum(diff * diff, axis=0) + 0.01))


def shift(x, axis, k, n):
    return lax.ppermute(x, axis, [(i, (i + k) % n) for i in range(n)])


def sum_over(x, axis, n):
    if n == 4:
        got = [shift(x, axis, k, n) for k in range(1, n)]
        even = lax.axis_index(axis) % 2 == 0
        first = x + jnp.where(even, got[2], got[0])
        second = got[1] + jnp.where(even, got[0], got[2])
        return first + second
    if n & (n - 1):
        return lax.psum(x, axis)
    step = 1
    while step < n:
        x = x + lax.ppermute(x, axis, [(i, i ^ step) for i in range(n)])
        step *= 2
    return x


def per_device(coords, lengthscales, vectors, mixing, noise):
    n_rows = coords.shape[1]
    local_tasks = vectors.shape[2]
    n_dp = lax.axis_size("dp")
    task_start = lax.axis_index("task") * local_tasks
    inverse = 1.0 / lengthscales
    own_scaled = coords.astype(jnp.float32) * inverse[:, None]

    def block(right_coords, values):
        right = right_coords.astype(jnp.float32) * inverse[:, None]
        tile = kernel_tile(own_scaled, right).astype(jnp.bfloat16)
        return jnp.einsum("nr,srm->snm", tile, values, preferred_element_type=jnp.float32)

    if n_dp <= 4:
        moved = [shift(vectors, "dp", k, n_dp) for k in range(1, n_dp)]
        summed = block(coords, vectors)
        for k in range(1, n_dp):
            summed = summed + block(shift(coords, "dp", k, n_dp), moved[k - 1])
    else:

        def ring(_, carry):
            accum, right_coords, values = carry
            right_coords = shift(right_coords, "dp", 1, n_dp)
            values = shift(values, "dp", 1, n_dp)
            return accum + block(right_coords, values), right_coords, values

        summed = block(coords, vectors)
        summed = lax.fori_loop(0, n_dp - 1, ring, (summed, coords, vectors))[0]

    whole_vectors = lax.all_gather(vectors, "task", axis=2, tiled=True)
    images = summed.astype(jnp.bfloat16)
    signs = jnp.array([1.0, -1.0], jnp.bfloat16)
    signed = images * signs[:, None, None]
    partial_grad = jnp.einsum(
        "sna,snb->ab", signed, whole_vectors, preferred_element_type=jnp.float32
    )
    total = sum_over(partial_grad, "dp", n_dp)
    whole_images = lax.all_gather(jnp.transpose(images, (2, 0, 1)), "task", axis=0, tiled=True)
    own_rows = lax.dynamic_slice_in_dim(mixing, task_start, local_tasks, 0)
    mixed = jnp.einsum("asn,ca->snc", whole_images, own_rows, preferred_element_type=jnp.float32)
    product = (mixed + noise[None, None, :] * vectors.astype(jnp.float32)).astype(jnp.bfloat16)
    gradient = total / (2.0 * n_rows * n_dp)
    return (product, gradient)


def solution(mesh):
    in_specs = (
        P(None, ("groups", "dp")),
        P("groups"),
        P(None, ("groups", "dp"), "task"),
        P("groups", None),
        P(("groups", "task")),
    )
    out_specs = (P(None, ("groups", "dp"), "task"), P(("groups", "task"), None))
    return jax.shard_map(
        per_device, mesh=mesh, in_specs=in_specs, out_specs=out_specs, check_vma=False
    )
```

```python
import jax
import jax.numpy as jnp
from jax import lax
from jax.experimental import pallas as pl
from jax.experimental.pallas import tpu as pltpu
from jax.sharding import PartitionSpec as P


def _block_kernel(rt_ref, l_ref, vt_ref, acc_ref, out_ref):
    n_cols = l_ref.shape[1]
    chunk = 256 if n_cols % 256 == 0 else n_cols
    for start in range(0, n_cols, chunk):
        cols = slice(start, start + chunk)
        d2 = None
        for c in range(rt_ref.shape[1]):
            diff = rt_ref[:, c : c + 1] - l_ref[c : c + 1, cols]
            d2 = diff * diff if d2 is None else d2 + diff * diff
        kt = jnp.exp(0.1 - jnp.sqrt(d2 + 0.01)).astype(jnp.bfloat16)
        for s in range(vt_ref.shape[0]):
            out_ref[s, :, cols] = acc_ref[s, :, cols] + jnp.dot(
                vt_ref[s], kt, preferred_element_type=jnp.float32
            )


def kernel_block(right_t, left, values_t, accum):
    r, n = right_t.shape[0], left.shape[1]
    s, t = values_t.shape[0], values_t.shape[1]
    vmem = pltpu.MemorySpace.VMEM if hasattr(pltpu, "MemorySpace") else pltpu.TPUMemorySpace.VMEM
    return pl.pallas_call(
        _block_kernel,
        out_shape=jax.ShapeDtypeStruct(accum.shape, jnp.float32),
        in_specs=[pl.BlockSpec(memory_space=vmem)] * 4,
        out_specs=pl.BlockSpec(memory_space=vmem),
        input_output_aliases={3: 0},
        cost_estimate=pl.CostEstimate(
            flops=2 * s * t * r * n + 10 * r * n,
            transcendentals=2 * r * n,
            bytes_accessed=4 * (r * 3 + 3 * n) + 2 * s * t * r + 8 * s * t * n,
        ),
    )(right_t, left, values_t, accum)


def shift(x, axis, k, n):
    return lax.ppermute(x, axis, [(i, (i + k) % n) for i in range(n)])


def sum_over(x, axis, n):
    if n == 4:
        got = [shift(x, axis, k, n) for k in range(1, n)]
        even = lax.axis_index(axis) % 2 == 0
        first = x + jnp.where(even, got[2], got[0])
        second = got[1] + jnp.where(even, got[0], got[2])
        return first + second
    if n & (n - 1):
        return lax.psum(x, axis)
    step = 1
    while step < n:
        x = x + lax.ppermute(x, axis, [(i, i ^ step) for i in range(n)])
        step *= 2
    return x


def per_device(coords, lengthscales, vectors, mixing, noise):
    n_rows = coords.shape[1]
    local_tasks = vectors.shape[2]
    n_dp = lax.axis_size("dp")
    task_start = lax.axis_index("task") * local_tasks
    inverse = 1.0 / lengthscales
    own_scaled = coords.astype(jnp.float32) * inverse[:, None]

    def block(accum, right_coords, values):
        right_t = (right_coords.astype(jnp.float32) * inverse[:, None]).T
        return kernel_block(right_t, own_scaled, jnp.swapaxes(values, 1, 2), accum)

    empty = jnp.zeros((vectors.shape[0], local_tasks, n_rows), jnp.float32)
    if n_dp <= 4:
        moved = [shift(vectors, "dp", k, n_dp) for k in range(1, n_dp)]
        summed = block(empty, coords, vectors)
        for k in range(1, n_dp):
            summed = block(summed, shift(coords, "dp", k, n_dp), moved[k - 1])
    else:

        def ring(_, carry):
            accum, right_coords, values = carry
            right_coords = shift(right_coords, "dp", 1, n_dp)
            values = shift(values, "dp", 1, n_dp)
            return block(accum, right_coords, values), right_coords, values

        summed = block(empty, coords, vectors)
        summed = lax.fori_loop(0, n_dp - 1, ring, (summed, coords, vectors))[0]
    summed = jnp.swapaxes(summed, 1, 2)

    whole_vectors = lax.all_gather(vectors, "task", axis=2, tiled=True)
    images = summed.astype(jnp.bfloat16)
    signs = jnp.array([1.0, -1.0], jnp.bfloat16)
    signed = images * signs[:, None, None]
    partial_grad = jnp.einsum(
        "sna,snb->ab", signed, whole_vectors, preferred_element_type=jnp.float32
    )
    total = sum_over(partial_grad, "dp", n_dp)
    whole_images = lax.all_gather(jnp.transpose(images, (2, 0, 1)), "task", axis=0, tiled=True)
    own_rows = lax.dynamic_slice_in_dim(mixing, task_start, local_tasks, 0)
    mixed = jnp.einsum("asn,ca->snc", whole_images, own_rows, preferred_element_type=jnp.float32)
    product = (mixed + noise[None, None, :] * vectors.astype(jnp.float32)).astype(jnp.bfloat16)
    gradient = total / (2.0 * n_rows * n_dp)
    return (product, gradient)


def solution(mesh):
    in_specs = (
        P(None, ("groups", "dp")),
        P("groups"),
        P(None, ("groups", "dp"), "task"),
        P("groups", None),
        P(("groups", "task")),
    )
    out_specs = (P(None, ("groups", "dp"), "task"), P(("groups", "task"), None))
    return jax.shard_map(
        per_device, mesh=mesh, in_specs=in_specs, out_specs=out_specs, check_vma=False
    )
```

```python
import jax
import jax.numpy as jnp
from jax import lax
from jax.sharding import PartitionSpec as P


def kernel_tile(left, right):
    diff = left[:, :, None] - right[:, None, :]
    return jnp.exp(0.1 - jnp.sqrt(jnp.sum(diff * diff, axis=0) + 0.01))


def shift(x, axis, k, n):
    return lax.ppermute(x, axis, [(i, (i + k) % n) for i in range(n)])


def sum_over(x, axis, n):
    if n == 4:
        got = [shift(x, axis, k, n) for k in range(1, n)]
        even = lax.axis_index(axis) % 2 == 0
        first = x + jnp.where(even, got[2], got[0])
        second = got[1] + jnp.where(even, got[0], got[2])
        return first + second
    if n & (n - 1):
        return lax.psum(x, axis)
    step = 1
    while step < n:
        x = x + lax.ppermute(x, axis, [(i, i ^ step) for i in range(n)])
        step *= 2
    return x


def per_device(coords, lengthscales, vectors, mixing, noise):
    n_rows = coords.shape[1]
    local_tasks = vectors.shape[2]
    n_dp = lax.axis_size("dp")
    task_start = lax.axis_index("task") * local_tasks
    inverse = 1.0 / lengthscales
    own_scaled = coords.astype(jnp.float32) * inverse[:, None]

    def block(right_coords, values):
        right = right_coords.astype(jnp.float32) * inverse[:, None]
        tile = kernel_tile(own_scaled, right).astype(jnp.bfloat16)
        return jnp.einsum("nr,srm->snm", tile, values, preferred_element_type=jnp.float32)

    if n_dp <= 4:
        moved = [shift(vectors, "dp", k, n_dp) for k in range(1, n_dp)]
        summed = block(coords, vectors)
        for k in range(1, n_dp):
            summed = summed + block(shift(coords, "dp", k, n_dp), moved[k - 1])
    else:

        def ring(_, carry):
            accum, right_coords, values = carry
            right_coords = shift(right_coords, "dp", 1, n_dp)
            values = shift(values, "dp", 1, n_dp)
            return accum + block(right_coords, values), right_coords, values

        summed = block(coords, vectors)
        summed = lax.fori_loop(0, n_dp - 1, ring, (summed, coords, vectors))[0]

    n_task = lax.axis_size("task")
    task_index = lax.axis_index("task")
    rotated = [vectors] + [shift(vectors, "task", -k, n_task) for k in range(1, n_task)]
    whole_vectors = jnp.concatenate(rotated, axis=2)
    images = summed.astype(jnp.bfloat16)
    signs = jnp.array([1.0, -1.0], jnp.bfloat16)
    signed = images * signs[:, None, None]
    partial_grad = jnp.einsum(
        "sna,snb->ab", signed, whole_vectors, preferred_element_type=jnp.float32
    )
    total = sum_over(partial_grad, "dp", n_dp)
    whole_images = lax.all_gather(jnp.transpose(images, (2, 0, 1)), "task", axis=0, tiled=True)
    own_rows = lax.dynamic_slice_in_dim(mixing, task_start, local_tasks, 0)
    mixed = jnp.einsum("asn,ca->snc", whole_images, own_rows, preferred_element_type=jnp.float32)
    product = (mixed + noise[None, None, :] * vectors.astype(jnp.float32)).astype(jnp.bfloat16)
    doubled = jnp.concatenate([total, total], axis=1)
    start = ((n_task - task_index) % n_task) * local_tasks
    total = lax.dynamic_slice_in_dim(doubled, start, n_task * local_tasks, 1)
    gradient = total / (2.0 * n_rows * n_dp)
    return (product, gradient)


def solution(mesh):
    in_specs = (
        P(None, ("groups", "dp")),
        P("groups"),
        P(None, ("groups", "dp"), "task"),
        P("groups", None),
        P(("groups", "task")),
    )
    out_specs = (P(None, ("groups", "dp"), "task"), P(("groups", "task"), None))
    return jax.shard_map(
        per_device, mesh=mesh, in_specs=in_specs, out_specs=out_specs, check_vma=False
    )
```

```python
import jax
import jax.numpy as jnp
from jax import lax
from jax.sharding import PartitionSpec as P


def kernel_tile(left, right):
    diff = left[:, :, None] - right[:, None, :]
    return jnp.exp(0.1 - jnp.sqrt(jnp.sum(diff * diff, axis=0) + 0.01))


def shift(x, axis, k, n):
    return lax.ppermute(x, axis, [(i, (i + k) % n) for i in range(n)])


def sum_over(x, axis, n):
    if n == 4:
        got = [shift(x, axis, k, n) for k in range(1, n)]
        even = lax.axis_index(axis) % 2 == 0
        first = x + jnp.where(even, got[2], got[0])
        second = got[1] + jnp.where(even, got[0], got[2])
        return first + second
    if n & (n - 1):
        return lax.psum(x, axis)
    step = 1
    while step < n:
        x = x + lax.ppermute(x, axis, [(i, i ^ step) for i in range(n)])
        step *= 2
    return x


def per_device(coords, lengthscales, vectors, mixing, noise):
    n_rows = coords.shape[1]
    local_tasks = vectors.shape[2]
    n_dp = lax.axis_size("dp")
    task_start = lax.axis_index("task") * local_tasks
    inverse = 1.0 / lengthscales
    own_scaled = coords.astype(jnp.float32) * inverse[:, None]

    def block(right_coords, values):
        right = right_coords.astype(jnp.float32) * inverse[:, None]
        tile = kernel_tile(own_scaled, right).astype(jnp.bfloat16)
        return jnp.einsum("nr,srm->snm", tile, values, preferred_element_type=jnp.float32)

    task_input = vectors
    if n_dp <= 4:
        moved = [shift(vectors, "dp", k, n_dp) for k in range(1, n_dp)]
        peer_coords = [shift(coords, "dp", k, n_dp) for k in range(1, n_dp)]
        task_input = lax.optimization_barrier((vectors, peer_coords))[0]
        summed = block(coords, vectors)
        for k in range(1, n_dp):
            summed = summed + block(peer_coords[k - 1], moved[k - 1])
    else:

        def ring(_, carry):
            accum, right_coords, values = carry
            right_coords = shift(right_coords, "dp", 1, n_dp)
            values = shift(values, "dp", 1, n_dp)
            return accum + block(right_coords, values), right_coords, values

        summed = block(coords, vectors)
        summed = lax.fori_loop(0, n_dp - 1, ring, (summed, coords, vectors))[0]

    whole_vectors = lax.all_gather(task_input, "task", axis=2, tiled=True)
    images = summed.astype(jnp.bfloat16)
    signs = jnp.array([1.0, -1.0], jnp.bfloat16)
    signed = images * signs[:, None, None]
    partial_grad = jnp.einsum(
        "sna,snb->ab", signed, whole_vectors, preferred_element_type=jnp.float32
    )
    total = sum_over(partial_grad, "dp", n_dp)
    whole_images = lax.all_gather(jnp.transpose(images, (2, 0, 1)), "task", axis=0, tiled=True)
    own_rows = lax.dynamic_slice_in_dim(mixing, task_start, local_tasks, 0)
    mixed = jnp.einsum("asn,ca->snc", whole_images, own_rows, preferred_element_type=jnp.float32)
    product = (mixed + noise[None, None, :] * vectors.astype(jnp.float32)).astype(jnp.bfloat16)
    gradient = total / (2.0 * n_rows * n_dp)
    return (product, gradient)


def solution(mesh):
    in_specs = (
        P(None, ("groups", "dp")),
        P("groups"),
        P(None, ("groups", "dp"), "task"),
        P("groups", None),
        P(("groups", "task")),
    )
    out_specs = (P(None, ("groups", "dp"), "task"), P(("groups", "task"), None))
    return jax.shard_map(
        per_device, mesh=mesh, in_specs=in_specs, out_specs=out_specs, check_vma=False
    )
```

```python
import jax
import jax.numpy as jnp
from jax import lax
from jax.sharding import PartitionSpec as P


def kernel_tile(left, right):
    total = None
    for c in range(left.shape[0]):
        diff = left[c][:, None] - right[c][None, :]
        total = diff * diff if total is None else total + diff * diff
    return jnp.exp(0.1 - jnp.sqrt(total + 0.01))


def shift(x, axis, k, n):
    return lax.ppermute(x, axis, [(i, (i + k) % n) for i in range(n)])


def sum_over(x, axis, n):
    if n == 4:
        got = [shift(x, axis, k, n) for k in range(1, n)]
        even = lax.axis_index(axis) % 2 == 0
        first = x + jnp.where(even, got[2], got[0])
        second = got[1] + jnp.where(even, got[0], got[2])
        return first + second
    if n & (n - 1):
        return lax.psum(x, axis)
    step = 1
    while step < n:
        x = x + lax.ppermute(x, axis, [(i, i ^ step) for i in range(n)])
        step *= 2
    return x


def per_device(coords, lengthscales, vectors, mixing, noise):
    n_rows = coords.shape[1]
    local_tasks = vectors.shape[2]
    n_dp = lax.axis_size("dp")
    task_start = lax.axis_index("task") * local_tasks
    inverse = 1.0 / lengthscales
    own_scaled = coords.astype(jnp.float32) * inverse[:, None]

    def block(right_coords, values):
        right = right_coords.astype(jnp.float32) * inverse[:, None]
        tile = kernel_tile(own_scaled, right).astype(jnp.bfloat16)
        return jnp.einsum("nr,srm->snm", tile, values, preferred_element_type=jnp.float32)

    task_input = vectors
    if n_dp <= 4:
        moved = [shift(vectors, "dp", k, n_dp) for k in range(1, n_dp)]
        peer_coords = [shift(coords, "dp", k, n_dp) for k in range(1, n_dp)]
        task_input = lax.optimization_barrier((vectors, peer_coords))[0]
        summed = block(coords, vectors)
        for k in range(1, n_dp):
            summed = summed + block(peer_coords[k - 1], moved[k - 1])
    else:

        def ring(_, carry):
            accum, right_coords, values = carry
            right_coords = shift(right_coords, "dp", 1, n_dp)
            values = shift(values, "dp", 1, n_dp)
            return accum + block(right_coords, values), right_coords, values

        summed = block(coords, vectors)
        summed = lax.fori_loop(0, n_dp - 1, ring, (summed, coords, vectors))[0]

    whole_vectors = lax.all_gather(task_input, "task", axis=2, tiled=True)
    images = summed.astype(jnp.bfloat16)
    signs = jnp.array([1.0, -1.0], jnp.bfloat16)
    signed = images * signs[:, None, None]
    partial_grad = jnp.einsum(
        "sna,snb->ab", signed, whole_vectors, preferred_element_type=jnp.float32
    )
    total = sum_over(partial_grad, "dp", n_dp)
    whole_images = lax.all_gather(jnp.transpose(images, (2, 0, 1)), "task", axis=0, tiled=True)
    own_rows = lax.dynamic_slice_in_dim(mixing, task_start, local_tasks, 0)
    mixed = jnp.einsum("asn,ca->snc", whole_images, own_rows, preferred_element_type=jnp.float32)
    product = (mixed + noise[None, None, :] * vectors.astype(jnp.float32)).astype(jnp.bfloat16)
    gradient = total / (2.0 * n_rows * n_dp)
    return (product, gradient)


def solution(mesh):
    in_specs = (
        P(None, ("groups", "dp")),
        P("groups"),
        P(None, ("groups", "dp"), "task"),
        P("groups", None),
        P(("groups", "task")),
    )
    out_specs = (P(None, ("groups", "dp"), "task"), P(("groups", "task"), None))
    return jax.shard_map(
        per_device, mesh=mesh, in_specs=in_specs, out_specs=out_specs, check_vma=False
    )
```

```python
import jax
import jax.numpy as jnp
from jax import lax
from jax.sharding import PartitionSpec as P


def kernel_tile(left, right):
    diff = left[:, :, None] - right[:, None, :]
    return jnp.exp(0.1 - jnp.sqrt(jnp.sum(diff * diff, axis=0) + 0.01))


def shift(x, axis, k, n):
    return lax.ppermute(x, axis, [(i, (i + k) % n) for i in range(n)])


def sum_over(x, axis, n):
    if n == 4:
        got = [shift(x, axis, k, n) for k in range(1, n)]
        even = lax.axis_index(axis) % 2 == 0
        first = x + jnp.where(even, got[2], got[0])
        second = got[1] + jnp.where(even, got[0], got[2])
        return first + second
    if n & (n - 1):
        return lax.psum(x, axis)
    step = 1
    while step < n:
        x = x + lax.ppermute(x, axis, [(i, i ^ step) for i in range(n)])
        step *= 2
    return x


def per_device(coords, lengthscales, vectors, mixing, noise):
    n_rows = coords.shape[1]
    local_tasks = vectors.shape[2]
    n_dp = lax.axis_size("dp")
    task_start = lax.axis_index("task") * local_tasks
    inverse = 1.0 / lengthscales
    own_scaled = coords.astype(jnp.float32) * inverse[:, None]

    def block(right_coords, values):
        right = right_coords.astype(jnp.float32) * inverse[:, None]
        tile = kernel_tile(own_scaled, right).astype(jnp.bfloat16)
        return jnp.einsum("nr,srm->snm", tile, values, preferred_element_type=jnp.float32)

    task_input = vectors
    if n_dp <= 4:
        summed, sent_vectors, sent_coords = lax.optimization_barrier(
            (block(coords, vectors), vectors, coords)
        )
        moved = [shift(sent_vectors, "dp", k, n_dp) for k in range(1, n_dp)]
        peer_coords = [shift(sent_coords, "dp", k, n_dp) for k in range(1, n_dp)]
        task_input = lax.optimization_barrier((vectors, peer_coords))[0]
        for k in range(1, n_dp):
            summed = summed + block(peer_coords[k - 1], moved[k - 1])
    else:

        def ring(_, carry):
            accum, right_coords, values = carry
            right_coords = shift(right_coords, "dp", 1, n_dp)
            values = shift(values, "dp", 1, n_dp)
            return accum + block(right_coords, values), right_coords, values

        summed = block(coords, vectors)
        summed = lax.fori_loop(0, n_dp - 1, ring, (summed, coords, vectors))[0]

    whole_vectors = lax.all_gather(task_input, "task", axis=2, tiled=True)
    images = summed.astype(jnp.bfloat16)
    signs = jnp.array([1.0, -1.0], jnp.bfloat16)
    signed = images * signs[:, None, None]
    partial_grad = jnp.einsum(
        "sna,snb->ab", signed, whole_vectors, preferred_element_type=jnp.float32
    )
    total = sum_over(partial_grad, "dp", n_dp)
    whole_images = lax.all_gather(jnp.transpose(images, (2, 0, 1)), "task", axis=0, tiled=True)
    own_rows = lax.dynamic_slice_in_dim(mixing, task_start, local_tasks, 0)
    mixed = jnp.einsum("asn,ca->snc", whole_images, own_rows, preferred_element_type=jnp.float32)
    product = (mixed + noise[None, None, :] * vectors.astype(jnp.float32)).astype(jnp.bfloat16)
    gradient = total / (2.0 * n_rows * n_dp)
    return (product, gradient)


def solution(mesh):
    in_specs = (
        P(None, ("groups", "dp")),
        P("groups"),
        P(None, ("groups", "dp"), "task"),
        P("groups", None),
        P(("groups", "task")),
    )
    out_specs = (P(None, ("groups", "dp"), "task"), P(("groups", "task"), None))
    return jax.shard_map(
        per_device, mesh=mesh, in_specs=in_specs, out_specs=out_specs, check_vma=False
    )
```

```python
import jax
import jax.numpy as jnp
from jax import lax
from jax.sharding import PartitionSpec as P


def kernel_tile(left, right):
    diff = left[:, :, None] - right[:, None, :]
    return jnp.exp(0.1 - jnp.sqrt(jnp.sum(diff * diff, axis=0) + 0.01))


def shift(x, axis, k, n):
    return lax.ppermute(x, axis, [(i, (i + k) % n) for i in range(n)])


def sum_over(x, axis, n):
    if n == 4:
        got = [shift(x, axis, k, n) for k in range(1, n)]
        even = lax.axis_index(axis) % 2 == 0
        first = x + jnp.where(even, got[2], got[0])
        second = got[1] + jnp.where(even, got[0], got[2])
        return first + second
    if n & (n - 1):
        return lax.psum(x, axis)
    step = 1
    while step < n:
        x = x + lax.ppermute(x, axis, [(i, i ^ step) for i in range(n)])
        step *= 2
    return x


def per_device(coords, lengthscales, vectors, mixing, noise):
    n_rows = coords.shape[1]
    local_tasks = vectors.shape[2]
    n_dp = lax.axis_size("dp")
    task_start = lax.axis_index("task") * local_tasks
    inverse = 1.0 / lengthscales
    own_scaled = coords.astype(jnp.float32) * inverse[:, None]

    def block(right_coords, values):
        right = right_coords.astype(jnp.float32) * inverse[:, None]
        tile = kernel_tile(own_scaled, right).astype(jnp.bfloat16)
        return jnp.einsum("nr,srm->snm", tile, values, preferred_element_type=jnp.float32)

    task_input = vectors
    if n_dp <= 4:
        moved = [shift(vectors, "dp", k, n_dp) for k in range(1, n_dp)]
        peer_coords = [shift(coords, "dp", k, n_dp) for k in range(1, n_dp)]
        task_input = lax.optimization_barrier((vectors, peer_coords))[0]
        summed = block(coords, vectors)
        for k in range(1, n_dp):
            summed = summed + block(peer_coords[k - 1], moved[k - 1])
    else:

        def ring(_, carry):
            accum, right_coords, values = carry
            right_coords = shift(right_coords, "dp", 1, n_dp)
            values = shift(values, "dp", 1, n_dp)
            return accum + block(right_coords, values), right_coords, values

        summed = block(coords, vectors)
        summed = lax.fori_loop(0, n_dp - 1, ring, (summed, coords, vectors))[0]

    n_task = lax.axis_size("task")
    task_index = lax.axis_index("task")
    if n_task == 4:
        partner = lax.ppermute(task_input, "task", [(i, i ^ 1) for i in range(4)])
        even = task_index % 2 == 0
        pair = jnp.concatenate(
            [jnp.where(even, task_input, partner), jnp.where(even, partner, task_input)], axis=2
        )
        other = lax.ppermute(pair, "task", [(i, i ^ 2) for i in range(4)])
        whole_vectors = jnp.concatenate([pair, other], axis=2)
    else:
        whole_vectors = lax.all_gather(task_input, "task", axis=2, tiled=True)
    images = summed.astype(jnp.bfloat16)
    signs = jnp.array([1.0, -1.0], jnp.bfloat16)
    signed = images * signs[:, None, None]
    partial_grad = jnp.einsum(
        "sna,snb->ab", signed, whole_vectors, preferred_element_type=jnp.float32
    )
    total = sum_over(partial_grad, "dp", n_dp)
    gather_input = lax.optimization_barrier((images, whole_vectors))[0]
    whole_images = lax.all_gather(jnp.transpose(gather_input, (2, 0, 1)), "task", axis=0, tiled=True)
    own_rows = lax.dynamic_slice_in_dim(mixing, task_start, local_tasks, 0)
    mixed = jnp.einsum("asn,ca->snc", whole_images, own_rows, preferred_element_type=jnp.float32)
    product = (mixed + noise[None, None, :] * vectors.astype(jnp.float32)).astype(jnp.bfloat16)
    if n_task == 4:
        half = 2 * local_tasks
        swapped = jnp.concatenate([total[:, half:], total[:, :half]], axis=1)
        total = jnp.where(task_index < 2, total, swapped)
    gradient = total / (2.0 * n_rows * n_dp)
    return (product, gradient)


def solution(mesh):
    in_specs = (
        P(None, ("groups", "dp")),
        P("groups"),
        P(None, ("groups", "dp"), "task"),
        P("groups", None),
        P(("groups", "task")),
    )
    out_specs = (P(None, ("groups", "dp"), "task"), P(("groups", "task"), None))
    return jax.shard_map(
        per_device, mesh=mesh, in_specs=in_specs, out_specs=out_specs, check_vma=False
    )
```

```python
import jax
import jax.numpy as jnp
from jax import lax
from jax.sharding import PartitionSpec as P


def kernel_tile(left, right):
    diff = left[:, :, None] - right[:, None, :]
    return jnp.exp(0.1 - jnp.sqrt(jnp.sum(diff * diff, axis=0) + 0.01))


def shift(x, axis, k, n):
    return lax.ppermute(x, axis, [(i, (i + k) % n) for i in range(n)])


def sum_over(x, axis, n):
    if n == 4:
        got = [shift(x, axis, k, n) for k in range(1, n)]
        even = lax.axis_index(axis) % 2 == 0
        first = x + jnp.where(even, got[2], got[0])
        second = got[1] + jnp.where(even, got[0], got[2])
        return first + second
    if n & (n - 1):
        return lax.psum(x, axis)
    step = 1
    while step < n:
        x = x + lax.ppermute(x, axis, [(i, i ^ step) for i in range(n)])
        step *= 2
    return x


def per_device(coords, lengthscales, vectors, mixing, noise):
    n_rows = coords.shape[1]
    local_tasks = vectors.shape[2]
    n_dp = lax.axis_size("dp")
    task_start = lax.axis_index("task") * local_tasks
    inverse = 1.0 / lengthscales
    own_scaled = coords.astype(jnp.float32) * inverse[:, None]

    def block(right_coords, values):
        right = right_coords.astype(jnp.float32) * inverse[:, None]
        tile = kernel_tile(own_scaled, right).astype(jnp.bfloat16)
        return jnp.einsum("nr,srm->snm", tile, values, preferred_element_type=jnp.float32)

    task_input = vectors
    if n_dp <= 4:
        moved = [shift(vectors, "dp", k, n_dp) for k in range(1, n_dp)]
        peer_coords = [shift(coords, "dp", k, n_dp) for k in range(1, n_dp)]
        task_input = lax.optimization_barrier((vectors, peer_coords))[0]
        summed = block(coords, vectors)
        for k in range(1, n_dp):
            summed = summed + block(peer_coords[k - 1], moved[k - 1])
    else:

        def ring(_, carry):
            accum, right_coords, values = carry
            right_coords = shift(right_coords, "dp", 1, n_dp)
            values = shift(values, "dp", 1, n_dp)
            return accum + block(right_coords, values), right_coords, values

        summed = block(coords, vectors)
        summed = lax.fori_loop(0, n_dp - 1, ring, (summed, coords, vectors))[0]

    n_task = lax.axis_size("task")
    copies = jnp.concatenate([task_input] * n_task, axis=2)
    whole_vectors = lax.all_to_all(copies, "task", 2, 2, tiled=True)
    images = summed.astype(jnp.bfloat16)
    signs = jnp.array([1.0, -1.0], jnp.bfloat16)
    signed = images * signs[:, None, None]
    partial_grad = jnp.einsum(
        "sna,snb->ab", signed, whole_vectors, preferred_element_type=jnp.float32
    )
    total = sum_over(partial_grad, "dp", n_dp)
    gather_input = lax.optimization_barrier((images, whole_vectors))[0]
    whole_images = lax.all_gather(jnp.transpose(gather_input, (2, 0, 1)), "task", axis=0, tiled=True)
    own_rows = lax.dynamic_slice_in_dim(mixing, task_start, local_tasks, 0)
    mixed = jnp.einsum("asn,ca->snc", whole_images, own_rows, preferred_element_type=jnp.float32)
    product = (mixed + noise[None, None, :] * vectors.astype(jnp.float32)).astype(jnp.bfloat16)
    gradient = total / (2.0 * n_rows * n_dp)
    return (product, gradient)


def solution(mesh):
    in_specs = (
        P(None, ("groups", "dp")),
        P("groups"),
        P(None, ("groups", "dp"), "task"),
        P("groups", None),
        P(("groups", "task")),
    )
    out_specs = (P(None, ("groups", "dp"), "task"), P(("groups", "task"), None))
    return jax.shard_map(
        per_device, mesh=mesh, in_specs=in_specs, out_specs=out_specs, check_vma=False
    )
```

```python
import jax
import jax.numpy as jnp
from jax import lax
from jax.sharding import PartitionSpec as P


def kernel_tile(left, right):
    diff = left[:, :, None] - right[:, None, :]
    return jnp.exp(0.1 - jnp.sqrt(jnp.sum(diff * diff, axis=0) + 0.01))


def shift(x, axis, k, n):
    return lax.ppermute(x, axis, [(i, (i + k) % n) for i in range(n)])


def sum_over(x, axis, n):
    if n == 4:
        got = [shift(x, axis, k, n) for k in range(1, n)]
        even = lax.axis_index(axis) % 2 == 0
        first = x + jnp.where(even, got[2], got[0])
        second = got[1] + jnp.where(even, got[0], got[2])
        return first + second
    if n & (n - 1):
        return lax.psum(x, axis)
    step = 1
    while step < n:
        x = x + lax.ppermute(x, axis, [(i, i ^ step) for i in range(n)])
        step *= 2
    return x


def per_device(coords, lengthscales, vectors, mixing, noise):
    n_rows = coords.shape[1]
    local_tasks = vectors.shape[2]
    n_dp = lax.axis_size("dp")
    task_start = lax.axis_index("task") * local_tasks
    inverse = 1.0 / lengthscales
    own_scaled = coords.astype(jnp.float32) * inverse[:, None]

    def block(right_coords, values):
        right = right_coords.astype(jnp.float32) * inverse[:, None]
        tile = kernel_tile(own_scaled, right).astype(jnp.bfloat16)
        return jnp.einsum("nr,srm->snm", tile, values, preferred_element_type=jnp.float32)

    task_input = vectors
    if n_dp <= 4:
        moved = [shift(vectors, "dp", k, n_dp) for k in range(1, n_dp)]
        peer_coords = [shift(coords, "dp", k, n_dp) for k in range(1, n_dp)]
        task_input = lax.optimization_barrier((vectors, peer_coords))[0]
        summed = block(coords, vectors)
        for k in range(1, n_dp):
            summed = summed + block(peer_coords[k - 1], moved[k - 1])
    else:

        def ring(_, carry):
            accum, right_coords, values = carry
            right_coords = shift(right_coords, "dp", 1, n_dp)
            values = shift(values, "dp", 1, n_dp)
            return accum + block(right_coords, values), right_coords, values

        summed = block(coords, vectors)
        summed = lax.fori_loop(0, n_dp - 1, ring, (summed, coords, vectors))[0]

    n_task = lax.axis_size("task")
    copies = jnp.broadcast_to(task_input[None], (n_task,) + vectors.shape)
    task_blocks = lax.all_to_all(copies, "task", 0, 0, tiled=True)
    images = summed.astype(jnp.bfloat16)
    signs = jnp.array([1.0, -1.0], jnp.bfloat16)
    signed = images * signs[:, None, None]
    partial_grad = jnp.einsum(
        "sna,ksnb->akb", signed, task_blocks, preferred_element_type=jnp.float32
    ).reshape(local_tasks, n_task * local_tasks)
    total = sum_over(partial_grad, "dp", n_dp)
    gather_input = lax.optimization_barrier((images, task_blocks))[0]
    whole_images = lax.all_gather(jnp.transpose(gather_input, (2, 0, 1)), "task", axis=0, tiled=True)
    own_rows = lax.dynamic_slice_in_dim(mixing, task_start, local_tasks, 0)
    mixed = jnp.einsum("asn,ca->snc", whole_images, own_rows, preferred_element_type=jnp.float32)
    product = (mixed + noise[None, None, :] * vectors.astype(jnp.float32)).astype(jnp.bfloat16)
    gradient = total / (2.0 * n_rows * n_dp)
    return (product, gradient)


def solution(mesh):
    in_specs = (
        P(None, ("groups", "dp")),
        P("groups"),
        P(None, ("groups", "dp"), "task"),
        P("groups", None),
        P(("groups", "task")),
    )
    out_specs = (P(None, ("groups", "dp"), "task"), P(("groups", "task"), None))
    return jax.shard_map(
        per_device, mesh=mesh, in_specs=in_specs, out_specs=out_specs, check_vma=False
    )
```

```python
import jax
import jax.numpy as jnp
from jax import lax
from jax.sharding import PartitionSpec as P


def kernel_tile(left, right):
    diff = left[:, :, None] - right[:, None, :]
    return jnp.exp(0.1 - jnp.sqrt(jnp.sum(diff * diff, axis=0) + 0.01))


def shift(x, axis, k, n):
    return lax.ppermute(x, axis, [(i, (i + k) % n) for i in range(n)])


def sum_over(x, axis, n):
    if n == 4:
        got = lax.all_to_all(jnp.broadcast_to(x[None], (n,) + x.shape), axis, 0, 0, tiled=True)
        return (got[0] + got[1]) + (got[2] + got[3])
    if n & (n - 1):
        return lax.psum(x, axis)
    step = 1
    while step < n:
        x = x + lax.ppermute(x, axis, [(i, i ^ step) for i in range(n)])
        step *= 2
    return x


def per_device(coords, lengthscales, vectors, mixing, noise):
    n_rows = coords.shape[1]
    local_tasks = vectors.shape[2]
    n_dp = lax.axis_size("dp")
    task_start = lax.axis_index("task") * local_tasks
    inverse = 1.0 / lengthscales
    own_scaled = coords.astype(jnp.float32) * inverse[:, None]

    def block(right_coords, values):
        right = right_coords.astype(jnp.float32) * inverse[:, None]
        tile = kernel_tile(own_scaled, right).astype(jnp.bfloat16)
        return jnp.einsum("nr,srm->snm", tile, values, preferred_element_type=jnp.float32)

    task_input = vectors
    if n_dp <= 4:
        moved = [shift(vectors, "dp", k, n_dp) for k in range(1, n_dp)]
        peer_coords = [shift(coords, "dp", k, n_dp) for k in range(1, n_dp)]
        task_input = lax.optimization_barrier((vectors, peer_coords))[0]
        summed = block(coords, vectors)
        for k in range(1, n_dp):
            summed = summed + block(peer_coords[k - 1], moved[k - 1])
    else:

        def ring(_, carry):
            accum, right_coords, values = carry
            right_coords = shift(right_coords, "dp", 1, n_dp)
            values = shift(values, "dp", 1, n_dp)
            return accum + block(right_coords, values), right_coords, values

        summed = block(coords, vectors)
        summed = lax.fori_loop(0, n_dp - 1, ring, (summed, coords, vectors))[0]

    n_task = lax.axis_size("task")
    copies = jnp.broadcast_to(task_input[None], (n_task,) + vectors.shape)
    task_blocks = lax.all_to_all(copies, "task", 0, 0, tiled=True)
    images = summed.astype(jnp.bfloat16)
    signs = jnp.array([1.0, -1.0], jnp.bfloat16)
    signed = images * signs[:, None, None]
    partial_grad = jnp.einsum(
        "sna,ksnb->akb", signed, task_blocks, preferred_element_type=jnp.float32
    ).reshape(local_tasks, n_task * local_tasks)
    total = sum_over(partial_grad, "dp", n_dp)
    gather_input = lax.optimization_barrier((images, task_blocks))[0]
    whole_images = lax.all_gather(jnp.transpose(gather_input, (2, 0, 1)), "task", axis=0, tiled=True)
    own_rows = lax.dynamic_slice_in_dim(mixing, task_start, local_tasks, 0)
    mixed = jnp.einsum("asn,ca->snc", whole_images, own_rows, preferred_element_type=jnp.float32)
    product = (mixed + noise[None, None, :] * vectors.astype(jnp.float32)).astype(jnp.bfloat16)
    gradient = total / (2.0 * n_rows * n_dp)
    return (product, gradient)


def solution(mesh):
    in_specs = (
        P(None, ("groups", "dp")),
        P("groups"),
        P(None, ("groups", "dp"), "task"),
        P("groups", None),
        P(("groups", "task")),
    )
    out_specs = (P(None, ("groups", "dp"), "task"), P(("groups", "task"), None))
    return jax.shard_map(
        per_device, mesh=mesh, in_specs=in_specs, out_specs=out_specs, check_vma=False
    )
```

```python
import jax
import jax.numpy as jnp
from jax import lax
from jax.sharding import PartitionSpec as P


def kernel_tile(left, right):
    diff = left[:, :, None] - right[:, None, :]
    return jnp.exp(0.1 - jnp.sqrt(jnp.sum(diff * diff, axis=0) + 0.01))


def shift(x, axis, k, n):
    return lax.ppermute(x, axis, [(i, (i + k) % n) for i in range(n)])


def sum_over(x, axis, n):
    if n == 4:
        got = [lax.ppermute(x, axis, [(i, i ^ k) for i in range(n)]) for k in range(1, n)]
        return (x + got[0]) + (got[1] + got[2])
    if n & (n - 1):
        return lax.psum(x, axis)
    step = 1
    while step < n:
        x = x + lax.ppermute(x, axis, [(i, i ^ step) for i in range(n)])
        step *= 2
    return x


def per_device(coords, lengthscales, vectors, mixing, noise):
    n_rows = coords.shape[1]
    local_tasks = vectors.shape[2]
    n_dp = lax.axis_size("dp")
    task_start = lax.axis_index("task") * local_tasks
    inverse = 1.0 / lengthscales
    own_scaled = coords.astype(jnp.float32) * inverse[:, None]

    def block(right_coords, values):
        right = right_coords.astype(jnp.float32) * inverse[:, None]
        tile = kernel_tile(own_scaled, right).astype(jnp.bfloat16)
        return jnp.einsum("nr,srm->snm", tile, values, preferred_element_type=jnp.float32)

    task_input = vectors
    if n_dp <= 4:
        moved = [shift(vectors, "dp", k, n_dp) for k in range(1, n_dp)]
        peer_coords = [shift(coords, "dp", k, n_dp) for k in range(1, n_dp)]
        task_input = lax.optimization_barrier((vectors, peer_coords))[0]
        summed = block(coords, vectors)
        for k in range(1, n_dp):
            summed = summed + block(peer_coords[k - 1], moved[k - 1])
    else:

        def ring(_, carry):
            accum, right_coords, values = carry
            right_coords = shift(right_coords, "dp", 1, n_dp)
            values = shift(values, "dp", 1, n_dp)
            return accum + block(right_coords, values), right_coords, values

        summed = block(coords, vectors)
        summed = lax.fori_loop(0, n_dp - 1, ring, (summed, coords, vectors))[0]

    n_task = lax.axis_size("task")
    copies = jnp.broadcast_to(task_input[None], (n_task,) + vectors.shape)
    task_blocks = lax.all_to_all(copies, "task", 0, 0, tiled=True)
    images = summed.astype(jnp.bfloat16)
    signs = jnp.array([1.0, -1.0], jnp.bfloat16)
    signed = images * signs[:, None, None]
    partial_grad = jnp.einsum(
        "sna,ksnb->akb", signed, task_blocks, preferred_element_type=jnp.float32
    ).reshape(local_tasks, n_task * local_tasks)
    total = sum_over(partial_grad, "dp", n_dp)
    gather_input = lax.optimization_barrier((images, task_blocks))[0]
    whole_images = lax.all_gather(jnp.transpose(gather_input, (2, 0, 1)), "task", axis=0, tiled=True)
    own_rows = lax.dynamic_slice_in_dim(mixing, task_start, local_tasks, 0)
    mixed = jnp.einsum("asn,ca->snc", whole_images, own_rows, preferred_element_type=jnp.float32)
    product = (mixed + noise[None, None, :] * vectors.astype(jnp.float32)).astype(jnp.bfloat16)
    gradient = total / (2.0 * n_rows * n_dp)
    return (product, gradient)


def solution(mesh):
    in_specs = (
        P(None, ("groups", "dp")),
        P("groups"),
        P(None, ("groups", "dp"), "task"),
        P("groups", None),
        P(("groups", "task")),
    )
    out_specs = (P(None, ("groups", "dp"), "task"), P(("groups", "task"), None))
    return jax.shard_map(
        per_device, mesh=mesh, in_specs=in_specs, out_specs=out_specs, check_vma=False
    )
```

```python
import jax
import jax.numpy as jnp
from jax import lax
from jax.sharding import PartitionSpec as P


def kernel_tile(left, right):
    diff = left[:, :, None] - right[:, None, :]
    return jnp.exp(0.1 - jnp.sqrt(jnp.sum(diff * diff, axis=0) + 0.01))


def shift(x, axis, k, n):
    return lax.ppermute(x, axis, [(i, (i + k) % n) for i in range(n)])


def sum_over(x, axis, n):
    if n == 4:
        got = [shift(x, axis, k, n) for k in range(1, n)]
        even = lax.axis_index(axis) % 2 == 0
        first = x + jnp.where(even, got[2], got[0])
        second = got[1] + jnp.where(even, got[0], got[2])
        return first + second
    if n & (n - 1):
        return lax.psum(x, axis)
    step = 1
    while step < n:
        x = x + lax.ppermute(x, axis, [(i, i ^ step) for i in range(n)])
        step *= 2
    return x


def per_device(coords, lengthscales, vectors, mixing, noise):
    n_rows = coords.shape[1]
    local_tasks = vectors.shape[2]
    n_dp = lax.axis_size("dp")
    task_start = lax.axis_index("task") * local_tasks
    inverse = 1.0 / lengthscales
    own_scaled = coords.astype(jnp.float32) * inverse[:, None]

    def block(right_coords, values):
        right = right_coords.astype(jnp.float32) * inverse[:, None]
        tile = kernel_tile(own_scaled, right).astype(jnp.bfloat16)
        return jnp.einsum("nr,srm->snm", tile, values, preferred_element_type=jnp.float32)

    task_input = vectors
    if n_dp <= 4:
        moved = [shift(vectors, "dp", k, n_dp) for k in range(1, n_dp)]
        peer_coords = [shift(coords, "dp", k, n_dp) for k in range(1, n_dp)]
        summed = block(coords, vectors)
        for k in range(1, n_dp):
            summed = summed + block(peer_coords[k - 1], moved[k - 1])
    else:

        def ring(_, carry):
            accum, right_coords, values = carry
            right_coords = shift(right_coords, "dp", 1, n_dp)
            values = shift(values, "dp", 1, n_dp)
            return accum + block(right_coords, values), right_coords, values

        summed = block(coords, vectors)
        summed = lax.fori_loop(0, n_dp - 1, ring, (summed, coords, vectors))[0]

    n_task = lax.axis_size("task")
    copies = jnp.broadcast_to(task_input[None], (n_task,) + vectors.shape)
    task_blocks = lax.all_to_all(copies, "task", 0, 0, tiled=True)
    images = summed.astype(jnp.bfloat16)
    signs = jnp.array([1.0, -1.0], jnp.bfloat16)
    signed = images * signs[:, None, None]
    partial_grad = jnp.einsum(
        "sna,ksnb->akb", signed, task_blocks, preferred_element_type=jnp.float32
    ).reshape(local_tasks, n_task * local_tasks)
    total = sum_over(partial_grad, "dp", n_dp)
    gather_input = lax.optimization_barrier((images, task_blocks))[0]
    whole_images = lax.all_gather(jnp.transpose(gather_input, (2, 0, 1)), "task", axis=0, tiled=True)
    own_rows = lax.dynamic_slice_in_dim(mixing, task_start, local_tasks, 0)
    mixed = jnp.einsum("asn,ca->snc", whole_images, own_rows, preferred_element_type=jnp.float32)
    product = (mixed + noise[None, None, :] * vectors.astype(jnp.float32)).astype(jnp.bfloat16)
    gradient = total / (2.0 * n_rows * n_dp)
    return (product, gradient)


def solution(mesh):
    in_specs = (
        P(None, ("groups", "dp")),
        P("groups"),
        P(None, ("groups", "dp"), "task"),
        P("groups", None),
        P(("groups", "task")),
    )
    out_specs = (P(None, ("groups", "dp"), "task"), P(("groups", "task"), None))
    return jax.shard_map(
        per_device, mesh=mesh, in_specs=in_specs, out_specs=out_specs, check_vma=False
    )
```

```python
import jax
import jax.numpy as jnp
from jax import lax
from jax.sharding import PartitionSpec as P


def kernel_tile(left, right):
    diff = left[:, :, None] - right[:, None, :]
    return jnp.exp(0.1 - jnp.sqrt(jnp.sum(diff * diff, axis=0) + 0.01))


def shift(x, axis, k, n):
    return lax.ppermute(x, axis, [(i, (i + k) % n) for i in range(n)])


def sum_over(x, axis, n):
    if n == 4:
        got = [shift(x, axis, k, n) for k in range(1, n)]
        even = lax.axis_index(axis) % 2 == 0
        first = x + jnp.where(even, got[2], got[0])
        second = got[1] + jnp.where(even, got[0], got[2])
        return first + second
    if n & (n - 1):
        return lax.psum(x, axis)
    step = 1
    while step < n:
        x = x + lax.ppermute(x, axis, [(i, i ^ step) for i in range(n)])
        step *= 2
    return x


def per_device(coords, lengthscales, vectors, mixing, noise):
    n_rows = coords.shape[1]
    local_tasks = vectors.shape[2]
    n_dp = lax.axis_size("dp")
    task_start = lax.axis_index("task") * local_tasks
    inverse = 1.0 / lengthscales
    own_scaled = coords.astype(jnp.float32) * inverse[:, None]

    def block(right_coords, values):
        right = right_coords.astype(jnp.float32) * inverse[:, None]
        tile = kernel_tile(own_scaled, right).astype(jnp.bfloat16)
        return jnp.einsum("nr,srm->snm", tile, values, preferred_element_type=jnp.float32)

    task_input = vectors
    if n_dp <= 4:
        moved = [shift(vectors, "dp", k, n_dp) for k in range(1, n_dp)]
        peer_coords = [shift(coords, "dp", k, n_dp) for k in range(1, n_dp)]
        task_input = lax.optimization_barrier((vectors, peer_coords))[0]
        summed = block(coords, vectors)
        for k in range(1, n_dp):
            summed = summed + block(peer_coords[k - 1], moved[k - 1])
    else:

        def ring(_, carry):
            accum, right_coords, values = carry
            right_coords = shift(right_coords, "dp", 1, n_dp)
            values = shift(values, "dp", 1, n_dp)
            return accum + block(right_coords, values), right_coords, values

        summed = block(coords, vectors)
        summed = lax.fori_loop(0, n_dp - 1, ring, (summed, coords, vectors))[0]

    n_task = lax.axis_size("task")
    copies = jnp.broadcast_to(task_input[None], (n_task,) + vectors.shape)
    task_blocks = lax.all_to_all(copies, "task", 0, 0, tiled=True)
    images = summed.astype(jnp.bfloat16)
    signs = jnp.array([1.0, -1.0], jnp.bfloat16)
    signed = images * signs[:, None, None]
    partial_grad = jnp.einsum(
        "sna,ksnb->akb", signed, task_blocks, preferred_element_type=jnp.float32
    ).reshape(local_tasks, n_task * local_tasks)
    total = sum_over(partial_grad, "dp", n_dp)
    gather_input = lax.optimization_barrier((images, task_blocks))[0]
    image_copies = jnp.broadcast_to(gather_input[None], (n_task,) + images.shape)
    image_blocks = lax.all_to_all(image_copies, "task", 0, 0, tiled=True)
    own_rows = lax.dynamic_slice_in_dim(mixing, task_start, local_tasks, 0)
    own_rows = own_rows.reshape(local_tasks, n_task, local_tasks)
    mixed = jnp.einsum("ksna,cka->snc", image_blocks, own_rows, preferred_element_type=jnp.float32)
    product = (mixed + noise[None, None, :] * vectors.astype(jnp.float32)).astype(jnp.bfloat16)
    gradient = total / (2.0 * n_rows * n_dp)
    return (product, gradient)


def solution(mesh):
    in_specs = (
        P(None, ("groups", "dp")),
        P("groups"),
        P(None, ("groups", "dp"), "task"),
        P("groups", None),
        P(("groups", "task")),
    )
    out_specs = (P(None, ("groups", "dp"), "task"), P(("groups", "task"), None))
    return jax.shard_map(
        per_device, mesh=mesh, in_specs=in_specs, out_specs=out_specs, check_vma=False
    )
```

```python
import jax
import jax.numpy as jnp
from jax import lax
from jax.sharding import PartitionSpec as P


def kernel_tile(left, right):
    diff = left[:, :, None] - right[:, None, :]
    return jnp.exp(0.1 - jnp.sqrt(jnp.sum(diff * diff, axis=0) + 0.01))


def shift(x, axis, k, n):
    return lax.ppermute(x, axis, [(i, (i + k) % n) for i in range(n)])


def sum_over(x, axis, n):
    if n == 4:
        got = [shift(x, axis, k, n) for k in range(1, n)]
        even = lax.axis_index(axis) % 2 == 0
        first = x + jnp.where(even, got[2], got[0])
        second = got[1] + jnp.where(even, got[0], got[2])
        return first + second
    if n & (n - 1):
        return lax.psum(x, axis)
    step = 1
    while step < n:
        x = x + lax.ppermute(x, axis, [(i, i ^ step) for i in range(n)])
        step *= 2
    return x


def per_device(coords, lengthscales, vectors, mixing, noise):
    n_rows = coords.shape[1]
    local_tasks = vectors.shape[2]
    n_dp = lax.axis_size("dp")
    task_start = lax.axis_index("task") * local_tasks
    inverse = 1.0 / lengthscales
    own_scaled = coords.astype(jnp.float32) * inverse[:, None]

    def block(right_coords, values):
        right = right_coords.astype(jnp.float32) * inverse[:, None]
        tile = kernel_tile(own_scaled, right).astype(jnp.bfloat16)
        return jnp.einsum("nr,srm->snm", tile, values, preferred_element_type=jnp.float32)

    task_input = vectors
    if n_dp <= 4:
        moved = [shift(vectors, "dp", k, n_dp) for k in range(1, n_dp)]
        peer_coords = [shift(coords, "dp", k, n_dp) for k in range(1, n_dp)]
        task_input = lax.optimization_barrier((vectors, peer_coords[0]))[0]
        summed = block(coords, vectors)
        for k in range(1, n_dp):
            summed = summed + block(peer_coords[k - 1], moved[k - 1])
    else:

        def ring(_, carry):
            accum, right_coords, values = carry
            right_coords = shift(right_coords, "dp", 1, n_dp)
            values = shift(values, "dp", 1, n_dp)
            return accum + block(right_coords, values), right_coords, values

        summed = block(coords, vectors)
        summed = lax.fori_loop(0, n_dp - 1, ring, (summed, coords, vectors))[0]

    n_task = lax.axis_size("task")
    copies = jnp.broadcast_to(task_input[None], (n_task,) + vectors.shape)
    task_blocks = lax.all_to_all(copies, "task", 0, 0, tiled=True)
    images = summed.astype(jnp.bfloat16)
    signs = jnp.array([1.0, -1.0], jnp.bfloat16)
    signed = images * signs[:, None, None]
    partial_grad = jnp.einsum(
        "sna,ksnb->akb", signed, task_blocks, preferred_element_type=jnp.float32
    ).reshape(local_tasks, n_task * local_tasks)
    total = sum_over(partial_grad, "dp", n_dp)
    gather_input = lax.optimization_barrier((images, task_blocks))[0]
    whole_images = lax.all_gather(jnp.transpose(gather_input, (2, 0, 1)), "task", axis=0, tiled=True)
    own_rows = lax.dynamic_slice_in_dim(mixing, task_start, local_tasks, 0)
    mixed = jnp.einsum("asn,ca->snc", whole_images, own_rows, preferred_element_type=jnp.float32)
    product = (mixed + noise[None, None, :] * vectors.astype(jnp.float32)).astype(jnp.bfloat16)
    gradient = total / (2.0 * n_rows * n_dp)
    return (product, gradient)


def solution(mesh):
    in_specs = (
        P(None, ("groups", "dp")),
        P("groups"),
        P(None, ("groups", "dp"), "task"),
        P("groups", None),
        P(("groups", "task")),
    )
    out_specs = (P(None, ("groups", "dp"), "task"), P(("groups", "task"), None))
    return jax.shard_map(
        per_device, mesh=mesh, in_specs=in_specs, out_specs=out_specs, check_vma=False
    )
```

```python
import jax
import jax.numpy as jnp
from jax import lax
from jax.sharding import PartitionSpec as P


def kernel_tile(left, right):
    diff = left[:, :, None] - right[:, None, :]
    return jnp.exp(0.1 - jnp.sqrt(jnp.sum(diff * diff, axis=0) + 0.01))


def shift(x, axis, k, n):
    return lax.ppermute(x, axis, [(i, (i + k) % n) for i in range(n)])


def sum_over(x, axis, n):
    if n == 4:
        got = [shift(x, axis, k, n) for k in range(1, n)]
        even = lax.axis_index(axis) % 2 == 0
        first = x + jnp.where(even, got[2], got[0])
        second = got[1] + jnp.where(even, got[0], got[2])
        return first + second
    if n & (n - 1):
        return lax.psum(x, axis)
    step = 1
    while step < n:
        x = x + lax.ppermute(x, axis, [(i, i ^ step) for i in range(n)])
        step *= 2
    return x


def per_device(coords, lengthscales, vectors, mixing, noise):
    n_rows = coords.shape[1]
    local_tasks = vectors.shape[2]
    n_dp = lax.axis_size("dp")
    task_start = lax.axis_index("task") * local_tasks
    inverse = 1.0 / lengthscales
    own_scaled = coords.astype(jnp.float32) * inverse[:, None]

    def block(right_coords, values):
        right = right_coords.astype(jnp.float32) * inverse[:, None]
        tile = kernel_tile(own_scaled, right).astype(jnp.bfloat16)
        return jnp.einsum("nr,srm->snm", tile, values, preferred_element_type=jnp.float32)

    task_input = vectors
    if n_dp <= 4:
        if n_dp & (n_dp - 1) == 0:
            def peer(x, k):
                return lax.ppermute(x, "dp", [(i, i ^ k) for i in range(n_dp)])
        else:

            def peer(x, k):
                return shift(x, "dp", k, n_dp)

        moved = [peer(vectors, k) for k in range(1, n_dp)]
        peer_coords = [peer(coords, k) for k in range(1, n_dp)]
        task_input = lax.optimization_barrier((vectors, peer_coords))[0]
        summed = block(coords, vectors)
        for k in range(1, n_dp):
            summed = summed + block(peer_coords[k - 1], moved[k - 1])
    else:

        def ring(_, carry):
            accum, right_coords, values = carry
            right_coords = shift(right_coords, "dp", 1, n_dp)
            values = shift(values, "dp", 1, n_dp)
            return accum + block(right_coords, values), right_coords, values

        summed = block(coords, vectors)
        summed = lax.fori_loop(0, n_dp - 1, ring, (summed, coords, vectors))[0]

    n_task = lax.axis_size("task")
    copies = jnp.broadcast_to(task_input[None], (n_task,) + vectors.shape)
    task_blocks = lax.all_to_all(copies, "task", 0, 0, tiled=True)
    images = summed.astype(jnp.bfloat16)
    signs = jnp.array([1.0, -1.0], jnp.bfloat16)
    signed = images * signs[:, None, None]
    partial_grad = jnp.einsum(
        "sna,ksnb->akb", signed, task_blocks, preferred_element_type=jnp.float32
    ).reshape(local_tasks, n_task * local_tasks)
    total = sum_over(partial_grad, "dp", n_dp)
    gather_input = lax.optimization_barrier((images, task_blocks))[0]
    whole_images = lax.all_gather(jnp.transpose(gather_input, (2, 0, 1)), "task", axis=0, tiled=True)
    own_rows = lax.dynamic_slice_in_dim(mixing, task_start, local_tasks, 0)
    mixed = jnp.einsum("asn,ca->snc", whole_images, own_rows, preferred_element_type=jnp.float32)
    product = (mixed + noise[None, None, :] * vectors.astype(jnp.float32)).astype(jnp.bfloat16)
    gradient = total / (2.0 * n_rows * n_dp)
    return (product, gradient)


def solution(mesh):
    in_specs = (
        P(None, ("groups", "dp")),
        P("groups"),
        P(None, ("groups", "dp"), "task"),
        P("groups", None),
        P(("groups", "task")),
    )
    out_specs = (P(None, ("groups", "dp"), "task"), P(("groups", "task"), None))
    return jax.shard_map(
        per_device, mesh=mesh, in_specs=in_specs, out_specs=out_specs, check_vma=False
    )
```

```python
import jax
import jax.numpy as jnp
from jax import lax
from jax.sharding import PartitionSpec as P


def kernel_tile(left, right):
    diff = left[:, :, None] - right[:, None, :]
    return jnp.exp(0.1 - jnp.sqrt(jnp.sum(diff * diff, axis=0) + 0.01))


def shift(x, axis, k, n):
    return lax.ppermute(x, axis, [(i, (i + k) % n) for i in range(n)])


def sum_over(x, axis, n):
    if n == 4:
        got = [shift(x, axis, k, n) for k in range(1, n)]
        even = lax.axis_index(axis) % 2 == 0
        first = x + jnp.where(even, got[2], got[0])
        second = got[1] + jnp.where(even, got[0], got[2])
        return first + second
    if n & (n - 1):
        return lax.psum(x, axis)
    step = 1
    while step < n:
        x = x + lax.ppermute(x, axis, [(i, i ^ step) for i in range(n)])
        step *= 2
    return x


def per_device(coords, lengthscales, vectors, mixing, noise):
    n_rows = coords.shape[1]
    local_tasks = vectors.shape[2]
    n_dp = lax.axis_size("dp")
    task_start = lax.axis_index("task") * local_tasks
    inverse = 1.0 / lengthscales
    own_scaled = coords.astype(jnp.float32) * inverse[:, None]

    def block(right_coords, values):
        right = right_coords.astype(jnp.float32) * inverse[:, None]
        tile = kernel_tile(own_scaled, right).astype(jnp.bfloat16)
        return jnp.einsum("nr,srm->snm", tile, values, preferred_element_type=jnp.float32)

    task_input = vectors
    if n_dp <= 4:
        moved = [shift(vectors, "dp", k, n_dp) for k in range(1, n_dp)]
        peer_coords = [shift(coords, "dp", k, n_dp) for k in range(1, n_dp)]
        task_input = lax.optimization_barrier((vectors, peer_coords))[0]
        summed = block(coords, vectors)
        if n_dp > 1:
            summed = summed + block(
                jnp.concatenate(peer_coords, axis=1), jnp.concatenate(moved, axis=1)
            )
    else:

        def ring(_, carry):
            accum, right_coords, values = carry
            right_coords = shift(right_coords, "dp", 1, n_dp)
            values = shift(values, "dp", 1, n_dp)
            return accum + block(right_coords, values), right_coords, values

        summed = block(coords, vectors)
        summed = lax.fori_loop(0, n_dp - 1, ring, (summed, coords, vectors))[0]

    n_task = lax.axis_size("task")
    copies = jnp.broadcast_to(task_input[None], (n_task,) + vectors.shape)
    task_blocks = lax.all_to_all(copies, "task", 0, 0, tiled=True)
    images = summed.astype(jnp.bfloat16)
    signs = jnp.array([1.0, -1.0], jnp.bfloat16)
    signed = images * signs[:, None, None]
    partial_grad = jnp.einsum(
        "sna,ksnb->akb", signed, task_blocks, preferred_element_type=jnp.float32
    ).reshape(local_tasks, n_task * local_tasks)
    total = sum_over(partial_grad, "dp", n_dp)
    gather_input = lax.optimization_barrier((images, task_blocks))[0]
    whole_images = lax.all_gather(jnp.transpose(gather_input, (2, 0, 1)), "task", axis=0, tiled=True)
    own_rows = lax.dynamic_slice_in_dim(mixing, task_start, local_tasks, 0)
    mixed = jnp.einsum("asn,ca->snc", whole_images, own_rows, preferred_element_type=jnp.float32)
    product = (mixed + noise[None, None, :] * vectors.astype(jnp.float32)).astype(jnp.bfloat16)
    gradient = total / (2.0 * n_rows * n_dp)
    return (product, gradient)


def solution(mesh):
    in_specs = (
        P(None, ("groups", "dp")),
        P("groups"),
        P(None, ("groups", "dp"), "task"),
        P("groups", None),
        P(("groups", "task")),
    )
    out_specs = (P(None, ("groups", "dp"), "task"), P(("groups", "task"), None))
    return jax.shard_map(
        per_device, mesh=mesh, in_specs=in_specs, out_specs=out_specs, check_vma=False
    )
```

```python
import jax
import jax.numpy as jnp
from jax import lax
from jax.sharding import PartitionSpec as P


def kernel_tile(left, right):
    diff = left[:, :, None] - right[:, None, :]
    return jnp.exp(0.1 - jnp.sqrt(jnp.sum(diff * diff, axis=0) + 0.01))


def shift(x, axis, k, n):
    return lax.ppermute(x, axis, [(i, (i + k) % n) for i in range(n)])


def sum_over(x, axis, n):
    if n == 4:
        got = [shift(x, axis, k, n) for k in range(1, n)]
        even = lax.axis_index(axis) % 2 == 0
        first = x + jnp.where(even, got[2], got[0])
        second = got[1] + jnp.where(even, got[0], got[2])
        return first + second
    if n & (n - 1):
        return lax.psum(x, axis)
    step = 1
    while step < n:
        x = x + lax.ppermute(x, axis, [(i, i ^ step) for i in range(n)])
        step *= 2
    return x


def per_device(coords, lengthscales, vectors, mixing, noise):
    n_rows = coords.shape[1]
    local_tasks = vectors.shape[2]
    n_dp = lax.axis_size("dp")
    task_start = lax.axis_index("task") * local_tasks
    inverse = 1.0 / lengthscales
    own_scaled = coords.astype(jnp.float32) * inverse[:, None]

    def block(right_coords, values, fused=False):
        right = right_coords.astype(jnp.float32) * inverse[:, None]
        if fused:
            total = None
            for c in range(right.shape[0]):
                diff = own_scaled[c][:, None] - right[c][None, :]
                total = diff * diff if total is None else total + diff * diff
            tile = jnp.exp(0.1 - jnp.sqrt(total + 0.01)).astype(jnp.bfloat16)
        else:
            tile = kernel_tile(own_scaled, right).astype(jnp.bfloat16)
        return jnp.einsum("nr,srm->snm", tile, values, preferred_element_type=jnp.float32)

    task_input = vectors
    if n_dp <= 4:
        moved = [shift(vectors, "dp", k, n_dp) for k in range(1, n_dp)]
        peer_coords = [shift(coords, "dp", k, n_dp) for k in range(1, n_dp)]
        task_input = lax.optimization_barrier((vectors, peer_coords))[0]
        summed = block(coords, vectors, fused=True)
        for k in range(1, n_dp):
            summed = summed + block(peer_coords[k - 1], moved[k - 1])
    else:

        def ring(_, carry):
            accum, right_coords, values = carry
            right_coords = shift(right_coords, "dp", 1, n_dp)
            values = shift(values, "dp", 1, n_dp)
            return accum + block(right_coords, values), right_coords, values

        summed = block(coords, vectors)
        summed = lax.fori_loop(0, n_dp - 1, ring, (summed, coords, vectors))[0]

    n_task = lax.axis_size("task")
    copies = jnp.broadcast_to(task_input[None], (n_task,) + vectors.shape)
    task_blocks = lax.all_to_all(copies, "task", 0, 0, tiled=True)
    images = summed.astype(jnp.bfloat16)
    signs = jnp.array([1.0, -1.0], jnp.bfloat16)
    signed = images * signs[:, None, None]
    partial_grad = jnp.einsum(
        "sna,ksnb->akb", signed, task_blocks, preferred_element_type=jnp.float32
    ).reshape(local_tasks, n_task * local_tasks)
    total = sum_over(partial_grad, "dp", n_dp)
    gather_input = lax.optimization_barrier((images, task_blocks))[0]
    whole_images = lax.all_gather(jnp.transpose(gather_input, (2, 0, 1)), "task", axis=0, tiled=True)
    own_rows = lax.dynamic_slice_in_dim(mixing, task_start, local_tasks, 0)
    mixed = jnp.einsum("asn,ca->snc", whole_images, own_rows, preferred_element_type=jnp.float32)
    product = (mixed + noise[None, None, :] * vectors.astype(jnp.float32)).astype(jnp.bfloat16)
    gradient = total / (2.0 * n_rows * n_dp)
    return (product, gradient)


def solution(mesh):
    in_specs = (
        P(None, ("groups", "dp")),
        P("groups"),
        P(None, ("groups", "dp"), "task"),
        P("groups", None),
        P(("groups", "task")),
    )
    out_specs = (P(None, ("groups", "dp"), "task"), P(("groups", "task"), None))
    return jax.shard_map(
        per_device, mesh=mesh, in_specs=in_specs, out_specs=out_specs, check_vma=False
    )
```

```python
import jax
import jax.numpy as jnp
from jax import lax
from jax.sharding import PartitionSpec as P


def kernel_tile(left, right):
    diff = left[:, :, None] - right[:, None, :]
    return jnp.exp(0.1 - jnp.sqrt(jnp.sum(diff * diff, axis=0) + 0.01))


def shift(x, axis, k, n):
    return lax.ppermute(x, axis, [(i, (i + k) % n) for i in range(n)])


def sum_over(x, axis, n):
    if n == 4:
        got = [shift(x, axis, k, n) for k in range(1, n)]
        even = lax.axis_index(axis) % 2 == 0
        first = x + jnp.where(even, got[2], got[0])
        second = got[1] + jnp.where(even, got[0], got[2])
        return first + second
    if n & (n - 1):
        return lax.psum(x, axis)
    step = 1
    while step < n:
        x = x + lax.ppermute(x, axis, [(i, i ^ step) for i in range(n)])
        step *= 2
    return x


def per_device(coords, lengthscales, vectors, mixing, noise):
    n_rows = coords.shape[1]
    local_tasks = vectors.shape[2]
    n_dp = lax.axis_size("dp")
    task_start = lax.axis_index("task") * local_tasks
    inverse = 1.0 / lengthscales
    own_scaled = coords.astype(jnp.float32) * inverse[:, None]

    def block(right_coords, values):
        right = right_coords.astype(jnp.float32) * inverse[:, None]
        tile = kernel_tile(own_scaled, right).astype(jnp.bfloat16)
        return jnp.einsum("nr,srm->snm", tile, values, preferred_element_type=jnp.float32)

    task_input = vectors
    if n_dp <= 4:
        moved = [shift(vectors, "dp", k, n_dp) for k in range(1, n_dp)]
        peer_coords = [shift(coords, "dp", k, n_dp) for k in range(1, n_dp)]
        task_input = lax.optimization_barrier((vectors, peer_coords))[0]
        summed = block(coords, vectors)
        order = [1, 3, 2] if n_dp == 4 else list(range(1, n_dp))
        for k in order:
            summed = summed + block(peer_coords[k - 1], moved[k - 1])
    else:

        def ring(_, carry):
            accum, right_coords, values = carry
            right_coords = shift(right_coords, "dp", 1, n_dp)
            values = shift(values, "dp", 1, n_dp)
            return accum + block(right_coords, values), right_coords, values

        summed = block(coords, vectors)
        summed = lax.fori_loop(0, n_dp - 1, ring, (summed, coords, vectors))[0]

    n_task = lax.axis_size("task")
    copies = jnp.broadcast_to(task_input[None], (n_task,) + vectors.shape)
    task_blocks = lax.all_to_all(copies, "task", 0, 0, tiled=True)
    images = summed.astype(jnp.bfloat16)
    signs = jnp.array([1.0, -1.0], jnp.bfloat16)
    signed = images * signs[:, None, None]
    partial_grad = jnp.einsum(
        "sna,ksnb->akb", signed, task_blocks, preferred_element_type=jnp.float32
    ).reshape(local_tasks, n_task * local_tasks)
    total = sum_over(partial_grad, "dp", n_dp)
    gather_input = lax.optimization_barrier((images, task_blocks))[0]
    whole_images = lax.all_gather(jnp.transpose(gather_input, (2, 0, 1)), "task", axis=0, tiled=True)
    own_rows = lax.dynamic_slice_in_dim(mixing, task_start, local_tasks, 0)
    mixed = jnp.einsum("asn,ca->snc", whole_images, own_rows, preferred_element_type=jnp.float32)
    product = (mixed + noise[None, None, :] * vectors.astype(jnp.float32)).astype(jnp.bfloat16)
    gradient = total / (2.0 * n_rows * n_dp)
    return (product, gradient)


def solution(mesh):
    in_specs = (
        P(None, ("groups", "dp")),
        P("groups"),
        P(None, ("groups", "dp"), "task"),
        P("groups", None),
        P(("groups", "task")),
    )
    out_specs = (P(None, ("groups", "dp"), "task"), P(("groups", "task"), None))
    return jax.shard_map(
        per_device, mesh=mesh, in_specs=in_specs, out_specs=out_specs, check_vma=False
    )
```

```python
import jax
import jax.numpy as jnp
from jax import lax
from jax.sharding import PartitionSpec as P


def kernel_tile(left, right):
    diff = left[:, :, None] - right[:, None, :]
    return jnp.exp(0.1 - jnp.sqrt(jnp.sum(diff * diff, axis=0) + 0.01))


def shift(x, axis, k, n):
    return lax.ppermute(x, axis, [(i, (i + k) % n) for i in range(n)])


def sum_over(x, axis, n):
    if n == 4:
        got = [shift(x, axis, k, n) for k in range(1, n)]
        even = lax.axis_index(axis) % 2 == 0
        first = x + jnp.where(even, got[2], got[0])
        second = got[1] + jnp.where(even, got[0], got[2])
        return first + second
    if n & (n - 1):
        return lax.psum(x, axis)
    step = 1
    while step < n:
        x = x + lax.ppermute(x, axis, [(i, i ^ step) for i in range(n)])
        step *= 2
    return x


def per_device(coords, lengthscales, vectors, mixing, noise):
    n_rows = coords.shape[1]
    local_tasks = vectors.shape[2]
    n_dp = lax.axis_size("dp")
    task_start = lax.axis_index("task") * local_tasks
    inverse = 1.0 / lengthscales
    own_scaled = coords.astype(jnp.float32) * inverse[:, None]

    def block(right_coords, values):
        right = right_coords.astype(jnp.float32) * inverse[:, None]
        tile = kernel_tile(own_scaled, right).astype(jnp.bfloat16)
        return jnp.einsum("nr,srm->snm", tile, values, preferred_element_type=jnp.float32)

    task_input = vectors
    if n_dp <= 4:
        moved = [shift(vectors, "dp", k, n_dp) for k in range(1, n_dp)]
        if n_dp == 4:
            first = shift(coords, "dp", 1, n_dp)
            peer_coords = [first, shift(first, "dp", 1, n_dp), shift(coords, "dp", 3, n_dp)]
        else:
            peer_coords = [shift(coords, "dp", k, n_dp) for k in range(1, n_dp)]
        task_input = lax.optimization_barrier((vectors, peer_coords))[0]
        summed = block(coords, vectors)
        order = [1, 3, 2] if n_dp == 4 else list(range(1, n_dp))
        for k in order:
            summed = summed + block(peer_coords[k - 1], moved[k - 1])
    else:

        def ring(_, carry):
            accum, right_coords, values = carry
            right_coords = shift(right_coords, "dp", 1, n_dp)
            values = shift(values, "dp", 1, n_dp)
            return accum + block(right_coords, values), right_coords, values

        summed = block(coords, vectors)
        summed = lax.fori_loop(0, n_dp - 1, ring, (summed, coords, vectors))[0]

    n_task = lax.axis_size("task")
    copies = jnp.broadcast_to(task_input[None], (n_task,) + vectors.shape)
    task_blocks = lax.all_to_all(copies, "task", 0, 0, tiled=True)
    images = summed.astype(jnp.bfloat16)
    signs = jnp.array([1.0, -1.0], jnp.bfloat16)
    signed = images * signs[:, None, None]
    partial_grad = jnp.einsum(
        "sna,ksnb->akb", signed, task_blocks, preferred_element_type=jnp.float32
    ).reshape(local_tasks, n_task * local_tasks)
    total = sum_over(partial_grad, "dp", n_dp)
    gather_input = lax.optimization_barrier((images, task_blocks))[0]
    whole_images = lax.all_gather(jnp.transpose(gather_input, (2, 0, 1)), "task", axis=0, tiled=True)
    own_rows = lax.dynamic_slice_in_dim(mixing, task_start, local_tasks, 0)
    mixed = jnp.einsum("asn,ca->snc", whole_images, own_rows, preferred_element_type=jnp.float32)
    product = (mixed + noise[None, None, :] * vectors.astype(jnp.float32)).astype(jnp.bfloat16)
    gradient = total / (2.0 * n_rows * n_dp)
    return (product, gradient)


def solution(mesh):
    in_specs = (
        P(None, ("groups", "dp")),
        P("groups"),
        P(None, ("groups", "dp"), "task"),
        P("groups", None),
        P(("groups", "task")),
    )
    out_specs = (P(None, ("groups", "dp"), "task"), P(("groups", "task"), None))
    return jax.shard_map(
        per_device, mesh=mesh, in_specs=in_specs, out_specs=out_specs, check_vma=False
    )
```

```python
import jax
import jax.numpy as jnp
from jax import lax
from jax.sharding import PartitionSpec as P


def kernel_tile(left, right):
    diff = left[:, :, None] - right[:, None, :]
    return jnp.exp(0.1 - jnp.sqrt(jnp.sum(diff * diff, axis=0) + 0.01))


def shift(x, axis, k, n):
    return lax.ppermute(x, axis, [(i, (i + k) % n) for i in range(n)])


def sum_over(x, axis, n):
    if n == 4:
        got = [lax.ppermute(x, axis, [(i, i ^ k) for i in range(n)]) for k in range(1, n)]
        return (x + got[0]) + (got[1] + got[2])
    if n & (n - 1):
        return lax.psum(x, axis)
    step = 1
    while step < n:
        x = x + lax.ppermute(x, axis, [(i, i ^ step) for i in range(n)])
        step *= 2
    return x


def per_device(coords, lengthscales, vectors, mixing, noise):
    n_rows = coords.shape[1]
    local_tasks = vectors.shape[2]
    n_dp = lax.axis_size("dp")
    task_start = lax.axis_index("task") * local_tasks
    inverse = 1.0 / lengthscales
    own_scaled = coords.astype(jnp.float32) * inverse[:, None]

    def block(right_coords, values):
        right = right_coords.astype(jnp.float32) * inverse[:, None]
        tile = kernel_tile(own_scaled, right).astype(jnp.bfloat16)
        return jnp.einsum("nr,srm->snm", tile, values, preferred_element_type=jnp.float32)

    task_input = vectors
    if n_dp <= 4:
        moved = [shift(vectors, "dp", k, n_dp) for k in range(1, n_dp)]
        peer_coords = [shift(coords, "dp", k, n_dp) for k in range(1, n_dp)]
        task_input = lax.optimization_barrier((vectors, peer_coords))[0]
        summed = block(coords, vectors)
        order = [1, 3, 2] if n_dp == 4 else list(range(1, n_dp))
        for k in order:
            summed = summed + block(peer_coords[k - 1], moved[k - 1])
    else:

        def ring(_, carry):
            accum, right_coords, values = carry
            right_coords = shift(right_coords, "dp", 1, n_dp)
            values = shift(values, "dp", 1, n_dp)
            return accum + block(right_coords, values), right_coords, values

        summed = block(coords, vectors)
        summed = lax.fori_loop(0, n_dp - 1, ring, (summed, coords, vectors))[0]

    n_task = lax.axis_size("task")
    copies = jnp.broadcast_to(task_input[None], (n_task,) + vectors.shape)
    task_blocks = lax.all_to_all(copies, "task", 0, 0, tiled=True)
    images = summed.astype(jnp.bfloat16)
    signs = jnp.array([1.0, -1.0], jnp.bfloat16)
    signed = images * signs[:, None, None]
    partial_grad = jnp.einsum(
        "sna,ksnb->akb", signed, task_blocks, preferred_element_type=jnp.float32
    ).reshape(local_tasks, n_task * local_tasks)
    total = sum_over(partial_grad, "dp", n_dp)
    gather_input = lax.optimization_barrier((images, task_blocks))[0]
    whole_images = lax.all_gather(jnp.transpose(gather_input, (2, 0, 1)), "task", axis=0, tiled=True)
    own_rows = lax.dynamic_slice_in_dim(mixing, task_start, local_tasks, 0)
    mixed = jnp.einsum("asn,ca->snc", whole_images, own_rows, preferred_element_type=jnp.float32)
    product = (mixed + noise[None, None, :] * vectors.astype(jnp.float32)).astype(jnp.bfloat16)
    gradient = total / (2.0 * n_rows * n_dp)
    return (product, gradient)


def solution(mesh):
    in_specs = (
        P(None, ("groups", "dp")),
        P("groups"),
        P(None, ("groups", "dp"), "task"),
        P("groups", None),
        P(("groups", "task")),
    )
    out_specs = (P(None, ("groups", "dp"), "task"), P(("groups", "task"), None))
    return jax.shard_map(
        per_device, mesh=mesh, in_specs=in_specs, out_specs=out_specs, check_vma=False
    )
```

```python
import jax
import jax.numpy as jnp
from jax import lax
from jax.sharding import PartitionSpec as P


def kernel_tile(left, right):
    diff = left[:, :, None] - right[:, None, :]
    return jnp.exp(0.1 - jnp.sqrt(jnp.sum(diff * diff, axis=0) + 0.01))


def shift(x, axis, k, n):
    return lax.ppermute(x, axis, [(i, (i + k) % n) for i in range(n)])


def sum_over(x, axis, n):
    if n == 4:
        got = [shift(x, axis, k, n) for k in range(1, n)]
        even = lax.axis_index(axis) % 2 == 0
        first = x + jnp.where(even, got[2], got[0])
        second = got[1] + jnp.where(even, got[0], got[2])
        return first + second
    if n & (n - 1):
        return lax.psum(x, axis)
    step = 1
    while step < n:
        x = x + lax.ppermute(x, axis, [(i, i ^ step) for i in range(n)])
        step *= 2
    return x


def per_device(coords, lengthscales, vectors, mixing, noise):
    n_rows = coords.shape[1]
    local_tasks = vectors.shape[2]
    n_dp = lax.axis_size("dp")
    task_start = lax.axis_index("task") * local_tasks
    inverse = 1.0 / lengthscales
    own_scaled = coords.astype(jnp.float32) * inverse[:, None]

    def block(right_coords, values):
        right = right_coords.astype(jnp.float32) * inverse[:, None]
        tile = kernel_tile(own_scaled, right).astype(jnp.bfloat16)
        return jnp.einsum("nr,srm->snm", tile, values, preferred_element_type=jnp.float32)

    task_input = vectors
    if n_dp <= 4:
        moved = [shift(vectors, "dp", k, n_dp) for k in range(1, n_dp)]
        peer_coords = [shift(coords, "dp", k, n_dp) for k in range(1, n_dp)]
        task_input = lax.optimization_barrier((vectors, peer_coords))[0]
        summed = block(coords, vectors)
        order = [3, 1, 2] if n_dp == 4 else list(range(1, n_dp))
        for k in order:
            summed = summed + block(peer_coords[k - 1], moved[k - 1])
    else:

        def ring(_, carry):
            accum, right_coords, values = carry
            right_coords = shift(right_coords, "dp", 1, n_dp)
            values = shift(values, "dp", 1, n_dp)
            return accum + block(right_coords, values), right_coords, values

        summed = block(coords, vectors)
        summed = lax.fori_loop(0, n_dp - 1, ring, (summed, coords, vectors))[0]

    n_task = lax.axis_size("task")
    copies = jnp.broadcast_to(task_input[None], (n_task,) + vectors.shape)
    task_blocks = lax.all_to_all(copies, "task", 0, 0, tiled=True)
    images = summed.astype(jnp.bfloat16)
    signs = jnp.array([1.0, -1.0], jnp.bfloat16)
    signed = images * signs[:, None, None]
    partial_grad = jnp.einsum(
        "sna,ksnb->akb", signed, task_blocks, preferred_element_type=jnp.float32
    ).reshape(local_tasks, n_task * local_tasks)
    total = sum_over(partial_grad, "dp", n_dp)
    gather_input = lax.optimization_barrier((images, task_blocks))[0]
    whole_images = lax.all_gather(jnp.transpose(gather_input, (2, 0, 1)), "task", axis=0, tiled=True)
    own_rows = lax.dynamic_slice_in_dim(mixing, task_start, local_tasks, 0)
    mixed = jnp.einsum("asn,ca->snc", whole_images, own_rows, preferred_element_type=jnp.float32)
    product = (mixed + noise[None, None, :] * vectors.astype(jnp.float32)).astype(jnp.bfloat16)
    gradient = total / (2.0 * n_rows * n_dp)
    return (product, gradient)


def solution(mesh):
    in_specs = (
        P(None, ("groups", "dp")),
        P("groups"),
        P(None, ("groups", "dp"), "task"),
        P("groups", None),
        P(("groups", "task")),
    )
    out_specs = (P(None, ("groups", "dp"), "task"), P(("groups", "task"), None))
    return jax.shard_map(
        per_device, mesh=mesh, in_specs=in_specs, out_specs=out_specs, check_vma=False
    )
```
